128 devices in a mesh: dp: 2 (over core), context: 4 (over z), tensor: 16 (over y, x).
Axes of the slice: x: 4, y: 4, z: 4, core: 2. Of those that a mesh axis runs over, the one named last changes fastest.
Arguments:
- tokens: bfloat16 [2, 2048, 8192], P('dp', ('context', 'tensor')), may hold values from -6 to 6
- filter_taps: float32 [2048, 8192], P(('context', 'tensor')), may hold values from -4.5 to 4.5
- query_weight: bfloat16 [32, 256, 256], P('tensor'), may hold values from -0.375 to 0.375
- key_weight: bfloat16 [32, 256, 256], P('tensor'), may hold values from -0.375 to 0.375
- value_weight: bfloat16 [32, 256, 256], P('tensor'), may hold values from -0.375 to 0.375
- output_weight: bfloat16 [32, 256, 256], P('tensor'), may hold values from -0.375 to 0.375
- out_cotangent: bfloat16 [2, 2048, 8192], P('dp', ('context', 'tensor')), may hold values from -6 to 6
Outputs:
- mixed: bfloat16 [2, 2048, 8192], P('dp', ('context', 'tensor'))
- token_grad: bfloat16 [2, 2048, 8192], P('dp', ('context', 'tensor'))
- filter_grad: float32 [2048, 8192], P(('context', 'tensor'))
- query_grad: float32 [32, 256, 256], P('tensor')
- key_grad: float32 [32, 256, 256], P('tensor')
- value_grad: float32 [32, 256, 256], P('tensor')
- output_grad: float32 [32, 256, 256], P('tensor')
The draws below stay inside these ranges and needn't reach their ends.
All inputs are finite; a program needn't handle non-finite values.
Results may differ from the reference program's by a relative error of at most 0.02.
Values may be sent and summed in bfloat16 or wider, within the bound.
No kernel may reach another device: no remote copies, remote signals or barrier semaphores. Data moves between devices by JAX's collectives and lax.ppermute only.
A program may use at most 128 MiB of HBM per device.

```python
import math
import jax
import jax.numpy as jnp
from jax import lax

D = 8192
BLK = 256
WINDOWS = 2
L = 2048
NBLK = 32


def draw_filter_taps(key, part):
    keys = jax.random.split(key, 4)
    lag = jnp.arange(L, dtype=jnp.float32)[:, None]
    rate = jnp.exp(jax.random.uniform(keys[0], (D,), jnp.float32, math.log(0.03 / L), math.log(1.0 / 30.0)))
    noise = jnp.clip(jax.random.normal(keys[1], (L, D), jnp.float32), -4.0, 4.0)
    spots = jax.random.randint(keys[2], (4,), 1, L)
    drops = jax.random.uniform(keys[3], (4, D), jnp.float32, 0.5, 0.8)
    envelope = jnp.exp(-rate[None, :] * lag)
    for index in range(4):
        envelope = envelope * jnp.where(lag >= spots[index].astype(jnp.float32), drops[index][None, :], 1.0)
    factor = jnp.sqrt((1.0 - jnp.exp(-2.0 * rate)) / (1.0 - jnp.exp(-2.0 * rate * L)))
    taps = noise * envelope * factor[None, :]
    return taps


def block_scale(own_key, dims, shards, low, high):
    level, own = 1.0, jax.random.fold_in(own_key, 6)
    for dim, blocks in shards:
        draws = jnp.exp(jax.random.uniform(jax.random.fold_in(own, dim), (blocks,), jnp.float32, low / len(shards), high / len(shards)))
        level = level * jnp.repeat(draws, dims[dim] // blocks).reshape([-1 if axis == dim else 1 for axis in range(len(dims))])
    return level


def bell_draw(own_key, dims, spread, reach, cuts=(), kind=jnp.bfloat16):
    drawn = jax.random.normal(own_key, dims, jnp.float32) * spread
    if len(cuts) > 0:
        drawn = block_scale(own_key, dims, cuts, -0.22, 0.18) * drawn
    return jnp.clip(drawn, min=-reach, max=reach).astype(kind)


def setup_inputs(seed: int = 0) -> dict:
    splits = jax.random.split(jax.random.key(seed), 8)
    return {
        "tokens": bell_draw(splits[0], (WINDOWS, L, D), 1.0, 6.0, ((0, 2), (1, 64))),
        "filter_taps": draw_filter_taps(jax.random.fold_in(splits[7], 71), 0),
        "query_weight": bell_draw(splits[2], (NBLK, BLK, BLK), BLK ** -0.5, 0.375, ((0, 16),)),
        "key_weight": bell_draw(splits[3], (NBLK, BLK, BLK), BLK ** -0.5, 0.375, ((0, 16),)),
        "value_weight": bell_draw(splits[4], (NBLK, BLK, BLK), BLK ** -0.5, 0.375, ((0, 16),)),
        "output_weight": bell_draw(splits[5], (NBLK, BLK, BLK), BLK ** -0.5, 0.375, ((0, 16),)),
        "out_cotangent": bell_draw(splits[6], (WINDOWS, L, D), 1.0, 6.0, ((0, 2), (1, 64))),
    }


def blockwise(acts, weight):
    rows = acts.shape[0]
    shaped = acts.reshape(rows, weight.shape[0], weight.shape[1]).astype(jnp.float32)
    return jnp.einsum('tni,nij->tnj', shaped, weight.astype(jnp.float32)).reshape(rows, -1)

def blockwise_back(acts, weight):
    rows = acts.shape[0]
    shaped = acts.reshape(rows, weight.shape[0], weight.shape[1]).astype(jnp.float32)
    return jnp.einsum('tnj,nij->tni', shaped, weight.astype(jnp.float32)).reshape(rows, -1)

def weight_term(inputs, grads, blocks):
    rows = inputs.shape[0]
    left = inputs.reshape(rows, blocks, -1).astype(jnp.float32)
    right = grads.reshape(rows, blocks, -1).astype(jnp.float32)
    return jnp.einsum('tni,tnj->nij', left, right)

def spectral_block(block):
    gated, conv_grad, taps = block
    length = gated.shape[0]
    size = 2 * length
    gated_spec = jnp.fft.rfft(gated, n=size, axis=0)
    grad_spec = jnp.fft.rfft(conv_grad, n=size, axis=0)
    taps_spec = jnp.fft.rfft(taps, n=size, axis=0)
    conv = jnp.fft.irfft(taps_spec * gated_spec, n=size, axis=0)[:length]
    gated_back = jnp.fft.irfft(jnp.conj(taps_spec) * grad_spec, n=size, axis=0)[:length]
    taps_back = jnp.fft.irfft(grad_spec * jnp.conj(gated_spec), n=size, axis=0)[:length]
    return (conv.astype(jnp.float32), gated_back.astype(jnp.float32), taps_back.astype(jnp.float32))

def to_blocks(array):
    return array.reshape(L, NBLK, BLK).transpose(1, 0, 2)

def from_blocks(array):
    return array.transpose(1, 0, 2).reshape(L, D)

def reference(tokens, filter_taps, query_weight, key_weight, value_weight, output_weight, out_cotangent):
    mixed_list = []
    token_list = []
    query_sum = jnp.zeros((NBLK, BLK, BLK), jnp.float32)
    key_sum = jnp.zeros((NBLK, BLK, BLK), jnp.float32)
    value_sum = jnp.zeros((NBLK, BLK, BLK), jnp.float32)
    output_sum = jnp.zeros((NBLK, BLK, BLK), jnp.float32)
    filter_sum = jnp.zeros((L, D), jnp.float32)
    taps_blocks = to_blocks(filter_taps.astype(jnp.float32))
    for window in range(WINDOWS):
        inputs = tokens[window]
        upstream = out_cotangent[window]
        query = blockwise(inputs, query_weight).astype(jnp.bfloat16)
        keys = blockwise(inputs, key_weight).astype(jnp.bfloat16)
        values = blockwise(inputs, value_weight).astype(jnp.bfloat16)
        gated = (keys.astype(jnp.float32) * values.astype(jnp.float32)).astype(jnp.bfloat16)
        back_weighted = blockwise_back(upstream, output_weight)
        conv_grad = (back_weighted * query.astype(jnp.float32)).astype(jnp.bfloat16)
        conv_b, gated_b, taps_b = lax.map(spectral_block, (to_blocks(gated.astype(jnp.float32)), to_blocks(conv_grad.astype(jnp.float32)), taps_blocks))
        conv = from_blocks(conv_b).astype(jnp.bfloat16)
        gated_back = from_blocks(gated_b).astype(jnp.bfloat16)
        filter_sum = filter_sum + from_blocks(taps_b)
        weighted = (query.astype(jnp.float32) * conv.astype(jnp.float32)).astype(jnp.bfloat16)
        mixed_list.append(blockwise(weighted, output_weight).astype(jnp.bfloat16))
        query_back = (back_weighted * conv.astype(jnp.float32)).astype(jnp.bfloat16)
        key_back = (gated_back.astype(jnp.float32) * values.astype(jnp.float32)).astype(jnp.bfloat16)
        value_back = (gated_back.astype(jnp.float32) * keys.astype(jnp.float32)).astype(jnp.bfloat16)
        token_grad = blockwise_back(query_back, query_weight) + blockwise_back(key_back, key_weight) + blockwise_back(value_back, value_weight)
        token_list.append(token_grad.astype(jnp.bfloat16))
        query_sum = query_sum + weight_term(inputs, query_back, NBLK)
        key_sum = key_sum + weight_term(inputs, key_back, NBLK)
        value_sum = value_sum + weight_term(inputs, value_back, NBLK)
        output_sum = output_sum + weight_term(weighted, upstream, NBLK)
    factor = 1.0 / math.sqrt(WINDOWS * L)
    return (jnp.stack(mixed_list), jnp.stack(token_list), filter_sum * factor, query_sum * factor, key_sum * factor, value_sum * factor, output_sum * factor)
```

```python
import math

import jax
import jax.numpy as jnp
from jax import lax
from jax.sharding import PartitionSpec as P

table_mode = lax.Precision.HIGH


def blockwise(acts, weight):
    rows = acts.shape[0]
    shaped = acts.reshape(rows, weight.shape[0], weight.shape[1])
    return jnp.einsum("tni,nij->tnj", shaped, weight, preferred_element_type=jnp.float32).reshape(
        rows, -1
    )


def blockwise_back(acts, weight):
    rows = acts.shape[0]
    shaped = acts.reshape(rows, weight.shape[0], weight.shape[1])
    return jnp.einsum("tnj,nij->tni", shaped, weight, preferred_element_type=jnp.float32).reshape(
        rows, -1
    )


def weight_term(inputs, grads, blocks):
    rows = inputs.shape[0]
    left = inputs.reshape(rows, blocks, -1)
    right = grads.reshape(rows, blocks, -1)
    return jnp.einsum("tni,tnj->nij", left, right, preferred_element_type=jnp.float32)


def angle_table(rows, cols, total):
    product = (
        jnp.arange(rows, dtype=jnp.int32)[:, None]
        * jnp.arange(cols, dtype=jnp.int32)[None, :]
        % total
    )
    angle = product.astype(jnp.float32) * (2.0 * math.pi / total)
    return (jnp.cos(angle), jnp.sin(angle))


def make_tables(length):
    second = length // 128
    cosine_first, sine_first = angle_table(128, 128, 128)
    cosine_second, sine_second = angle_table(second, second, second)
    cosine_twist, sine_twist = angle_table(128, second, length)
    return (
        cosine_first,
        sine_first,
        cosine_second,
        sine_second,
        cosine_twist[:, :, None],
        sine_twist[:, :, None],
    )


def across_first(matrix, array):
    return jnp.einsum(
        "kn,nmc->kmc", matrix, array, precision=table_mode, preferred_element_type=jnp.float32
    )


def across_second(array, matrix):
    return jnp.einsum(
        "kmc,ml->klc", array, matrix, precision=table_mode, preferred_element_type=jnp.float32
    )


def forward_transform(signal, tables):
    cosine_first, sine_first, cosine_second, sine_second, cosine_twist, sine_twist = tables
    half = cosine_first.shape[0] // 2
    shaped = signal.reshape(half, cosine_second.shape[0], signal.shape[1])
    real_section = across_first(cosine_first[:, :half], shaped)
    imag_section = -across_first(sine_first[:, :half], shaped)
    real_turned = real_section * cosine_twist + imag_section * sine_twist
    imag_turned = imag_section * cosine_twist - real_section * sine_twist
    real_out = across_second(real_turned, cosine_second) + across_second(imag_turned, sine_second)
    imag_out = across_second(imag_turned, cosine_second) - across_second(real_turned, sine_second)
    return (real_out, imag_out)


def inverse_transform(real_spec, imag_spec, tables):
    cosine_first, sine_first, cosine_second, sine_second, cosine_twist, sine_twist = tables
    half = cosine_first.shape[0] // 2
    total = cosine_first.shape[0] * cosine_second.shape[0]
    real_section = across_second(real_spec, cosine_second) - across_second(imag_spec, sine_second)
    imag_section = across_second(imag_spec, cosine_second) + across_second(real_spec, sine_second)
    real_turned = real_section * cosine_twist - imag_section * sine_twist
    imag_turned = imag_section * cosine_twist + real_section * sine_twist
    signal = (
        across_first(cosine_first[:half], real_turned)
        - across_first(sine_first[:half], imag_turned)
    ) / total
    return signal.reshape(half * cosine_second.shape[0], -1)


def shards(
    tokens, filter_taps, query_weight, key_weight, value_weight, output_weight, out_cotangent
):
    ctx = lax.axis_size("context")
    ten = lax.axis_size("tensor")
    both = lax.all_to_all(
        jnp.stack([tokens[0], out_cotangent[0]]), "tensor", split_axis=2, concat_axis=1, tiled=True
    )
    inputs, upstream = both[0], both[1]
    blocks = query_weight.shape[0]
    query = blockwise(inputs, query_weight).astype(jnp.bfloat16)
    keys = blockwise(inputs, key_weight).astype(jnp.bfloat16)
    values = blockwise(inputs, value_weight).astype(jnp.bfloat16)
    gated = (keys.astype(jnp.float32) * values.astype(jnp.float32)).astype(jnp.bfloat16)
    query_wide = query.astype(jnp.float32)
    rows, width = filter_taps.shape
    taps_order = (
        filter_taps.reshape(rows, ten, ctx, width // (ten * ctx))
        .transpose(0, 2, 1, 3)
        .reshape(rows, width)
    )
    taps = lax.all_to_all(
        taps_order, ("context", "tensor"), split_axis=1, concat_axis=0, tiled=True
    )
    length = taps.shape[0]
    tables = make_tables(2 * length)
    back_weighted = blockwise_back(upstream, output_weight)
    conv_grad = (back_weighted * query_wide).astype(jnp.bfloat16)
    pair_time = lax.all_to_all(
        jnp.stack([gated, conv_grad]), "context", split_axis=2, concat_axis=1, tiled=True
    )
    gated_time, grad_time = pair_time[0], pair_time[1]
    real_taps, imag_taps = forward_transform(taps, tables)
    real_gated, imag_gated = forward_transform(gated_time.astype(jnp.float32), tables)
    conv_time = inverse_transform(
        real_taps * real_gated - imag_taps * imag_gated,
        real_taps * imag_gated + imag_taps * real_gated,
        tables,
    )
    real_grad, imag_grad = forward_transform(grad_time.astype(jnp.float32), tables)
    gated_time_back = inverse_transform(
        real_taps * real_grad + imag_taps * imag_grad,
        real_taps * imag_grad - imag_taps * real_grad,
        tables,
    )
    taps_back = inverse_transform(
        real_grad * real_gated + imag_grad * imag_gated,
        imag_grad * real_gated - real_grad * imag_gated,
        tables,
    )
    pair_back = lax.all_to_all(
        jnp.stack([conv_time.astype(jnp.bfloat16), gated_time_back.astype(jnp.bfloat16)]),
        "context",
        split_axis=1,
        concat_axis=2,
        tiled=True,
    )
    conv, gated_narrow = pair_back[0], pair_back[1]
    conv_wide = conv.astype(jnp.float32)
    weighted = (query_wide * conv_wide).astype(jnp.bfloat16)
    mixed = blockwise(weighted, output_weight).astype(jnp.bfloat16)
    query_back = (back_weighted * conv_wide).astype(jnp.bfloat16)
    gated_back = gated_narrow.astype(jnp.float32)
    key_back = (gated_back * values.astype(jnp.float32)).astype(jnp.bfloat16)
    value_back = (gated_back * keys.astype(jnp.float32)).astype(jnp.bfloat16)
    token_grad = (
        blockwise_back(query_back, query_weight)
        + blockwise_back(key_back, key_weight)
        + blockwise_back(value_back, value_weight)
    ).astype(jnp.bfloat16)
    factor = 1.0 / math.sqrt(lax.axis_size("dp") * length)
    query_grad, key_grad, value_grad, output_grad = (
        lax.psum(
            (weight_term(inputs, query_back, blocks) * factor).astype(jnp.bfloat16),
            ("dp", "context"),
        ).astype(jnp.float32),
        lax.psum(
            (weight_term(inputs, key_back, blocks) * factor).astype(jnp.bfloat16), ("dp", "context")
        ).astype(jnp.float32),
        lax.psum(
            (weight_term(inputs, value_back, blocks) * factor).astype(jnp.bfloat16),
            ("dp", "context"),
        ).astype(jnp.float32),
        lax.psum(
            (weight_term(weighted, upstream, blocks) * factor).astype(jnp.bfloat16),
            ("dp", "context"),
        ).astype(jnp.float32),
    )
    taps_total = lax.psum((taps_back * factor).astype(jnp.bfloat16), "dp")
    spread = lax.all_to_all(
        taps_total, ("context", "tensor"), split_axis=0, concat_axis=1, tiled=True
    )
    out_rows = spread.shape[0]
    filter_grad = (
        spread.reshape(out_rows, ctx, ten, width // (ten * ctx))
        .transpose(0, 2, 1, 3)
        .reshape(out_rows, width)
        .astype(jnp.float32)
    )
    rows_pair = lax.all_to_all(
        jnp.stack([mixed, token_grad]), "tensor", split_axis=1, concat_axis=2, tiled=True
    )
    return (
        rows_pair[0][None],
        rows_pair[1][None],
        filter_grad,
        query_grad,
        key_grad,
        value_grad,
        output_grad,
    )


def solution(mesh):
    placed = (
        P("dp", ("context", "tensor"), None),
        P(("context", "tensor"), None),
        P("tensor", None, None),
        P("tensor", None, None),
        P("tensor", None, None),
        P("tensor", None, None),
        P("dp", ("context", "tensor"), None),
    )
    return jax.shard_map(
        shards,
        mesh=mesh,
        in_specs=placed,
        out_specs=(
            P("dp", ("context", "tensor"), None),
            P("dp", ("context", "tensor"), None),
            P(("context", "tensor"), None),
            P("tensor", None, None),
            P("tensor", None, None),
            P("tensor", None, None),
            P("tensor", None, None),
        ),
        check_vma=False,
    )
```

```python
import math

import jax
import jax.numpy as jnp
from jax import lax
from jax.sharding import PartitionSpec as P

table_mode = lax.Precision.HIGH


def blockwise(acts, weight):
    rows = acts.shape[0]
    shaped = acts.reshape(rows, weight.shape[0], weight.shape[1])
    return jnp.einsum("tni,nij->tnj", shaped, weight, preferred_element_type=jnp.float32).reshape(
        rows, -1
    )


def blockwise_back(acts, weight):
    rows = acts.shape[0]
    shaped = acts.reshape(rows, weight.shape[0], weight.shape[1])
    return jnp.einsum("tnj,nij->tni", shaped, weight, preferred_element_type=jnp.float32).reshape(
        rows, -1
    )


def weight_term(inputs, grads, blocks):
    rows = inputs.shape[0]
    left = inputs.reshape(rows, blocks, -1)
    right = grads.reshape(rows, blocks, -1)
    return jnp.einsum("tni,tnj->nij", left, right, preferred_element_type=jnp.float32)


def angle_table(rows, cols, total):
    product = (
        jnp.arange(rows, dtype=jnp.int32)[:, None]
        * jnp.arange(cols, dtype=jnp.int32)[None, :]
        % total
    )
    angle = product.astype(jnp.float32) * (2.0 * math.pi / total)
    return (jnp.cos(angle), jnp.sin(angle))


def make_tables(length):
    second = length // 128
    cosine_first, sine_first = angle_table(128, 128, 128)
    cosine_second, sine_second = angle_table(second, second, second)
    cosine_twist, sine_twist = angle_table(128, second, length)
    return (
        cosine_first,
        sine_first,
        cosine_second,
        sine_second,
        cosine_twist[:, :, None],
        sine_twist[:, :, None],
    )


def across_first(matrix, array):
    return jnp.einsum(
        "kn,nmc->kmc", matrix, array, precision=table_mode, preferred_element_type=jnp.float32
    )


def across_second(array, matrix):
    return jnp.einsum(
        "kmc,ml->klc", array, matrix, precision=table_mode, preferred_element_type=jnp.float32
    )


def forward_transform(signal, tables):
    cosine_first, sine_first, cosine_second, sine_second, cosine_twist, sine_twist = tables
    half = cosine_first.shape[0] // 2
    shaped = signal.reshape(half, cosine_second.shape[0], signal.shape[1])
    real_section = across_first(cosine_first[:, :half], shaped)
    imag_section = -across_first(sine_first[:, :half], shaped)
    real_turned = real_section * cosine_twist + imag_section * sine_twist
    imag_turned = imag_section * cosine_twist - real_section * sine_twist
    real_out = across_second(real_turned, cosine_second) + across_second(imag_turned, sine_second)
    imag_out = across_second(imag_turned, cosine_second) - across_second(real_turned, sine_second)
    return (real_out, imag_out)


def inverse_transform(real_spec, imag_spec, tables):
    cosine_first, sine_first, cosine_second, sine_second, cosine_twist, sine_twist = tables
    half = cosine_first.shape[0] // 2
    total = cosine_first.shape[0] * cosine_second.shape[0]
    real_section = across_second(real_spec, cosine_second) - across_second(imag_spec, sine_second)
    imag_section = across_second(imag_spec, cosine_second) + across_second(real_spec, sine_second)
    real_turned = real_section * cosine_twist - imag_section * sine_twist
    imag_turned = imag_section * cosine_twist + real_section * sine_twist
    signal = (
        across_first(cosine_first[:half], real_turned)
        - across_first(sine_first[:half], imag_turned)
    ) / total
    return signal.reshape(half * cosine_second.shape[0], -1)


def spectral_tables(length):
    first = 128
    second = length // first
    half = first // 2
    cosine_first, sine_first = angle_table(first, first, first)
    cosine_second, sine_second = angle_table(second, second, second)
    cosine_twist, sine_twist = angle_table(first, second, length)
    forward_first = jnp.concatenate([cosine_first[:, :half], -sine_first[:, :half]], axis=0)
    forward_second = jnp.stack(
        [
            jnp.stack([cosine_second, -sine_second], axis=1),
            jnp.stack([sine_second, cosine_second], axis=1),
        ]
    )
    inverse_second = jnp.stack(
        [
            jnp.stack([cosine_second, sine_second], axis=1),
            jnp.stack([-sine_second, cosine_second], axis=1),
        ]
    )
    inverse_first = jnp.stack([cosine_first[:half], -sine_first[:half]], axis=1) / length
    return (
        forward_first,
        forward_second,
        inverse_second,
        inverse_first,
        cosine_twist[:, :, None],
        sine_twist[:, :, None],
    )


def spectra(signal, tables):
    forward_first, forward_second, _, _, cosine_twist, sine_twist = tables
    first = cosine_twist.shape[0]
    half = first // 2
    shaped = signal.reshape(half, cosine_twist.shape[1], signal.shape[1])
    section = jnp.einsum(
        "kn,nmc->kmc", forward_first, shaped, precision=table_mode,
        preferred_element_type=jnp.float32,
    )
    real_section, imag_section = section[:first], section[first:]
    turned = jnp.stack(
        [
            real_section * cosine_twist + imag_section * sine_twist,
            imag_section * cosine_twist - real_section * sine_twist,
        ]
    )
    return jnp.einsum(
        "rkmc,rmsl->sklc", turned, forward_second, precision=table_mode,
        preferred_element_type=jnp.float32,
    )


def signals(spec, tables):
    _, _, inverse_second, inverse_first, cosine_twist, sine_twist = tables
    section = jnp.einsum(
        "sklc,slrm->rkmc", spec, inverse_second, precision=table_mode,
        preferred_element_type=jnp.float32,
    )
    real_section, imag_section = section[0], section[1]
    turned = jnp.stack(
        [
            real_section * cosine_twist - imag_section * sine_twist,
            imag_section * cosine_twist + real_section * sine_twist,
        ]
    )
    out = jnp.einsum(
        "nrk,rkmc->nmc", inverse_first, turned, precision=table_mode,
        preferred_element_type=jnp.float32,
    )
    return out.reshape(-1, out.shape[-1])


def shards(
    tokens, filter_taps, query_weight, key_weight, value_weight, output_weight, out_cotangent
):
    inputs, upstream = (
        lax.all_to_all(tokens[0], "tensor", split_axis=1, concat_axis=0, tiled=True),
        lax.all_to_all(out_cotangent[0], "tensor", split_axis=1, concat_axis=0, tiled=True),
    )
    blocks = query_weight.shape[0]
    query = blockwise(inputs, query_weight).astype(jnp.bfloat16)
    keys = blockwise(inputs, key_weight).astype(jnp.bfloat16)
    values = blockwise(inputs, value_weight).astype(jnp.bfloat16)
    gated = (keys.astype(jnp.float32) * values.astype(jnp.float32)).astype(jnp.bfloat16)
    query_wide = query.astype(jnp.float32)
    taps = lax.all_to_all(
        lax.all_to_all(filter_taps, "tensor", split_axis=1, concat_axis=0, tiled=True),
        "context",
        split_axis=1,
        concat_axis=0,
        tiled=True,
    )
    length = taps.shape[0]
    width = taps.shape[1]
    tables = spectral_tables(2 * length)
    gated_time = lax.all_to_all(gated, "context", split_axis=1, concat_axis=0, tiled=True)
    back_weighted = blockwise_back(upstream, output_weight)
    conv_grad = (back_weighted * query_wide).astype(jnp.bfloat16)
    grad_time = lax.all_to_all(conv_grad, "context", split_axis=1, concat_axis=0, tiled=True)
    spec = spectra(
        jnp.concatenate(
            [taps, gated_time.astype(jnp.float32), grad_time.astype(jnp.float32)], axis=1
        ),
        tables,
    )
    real_spec, imag_spec = spec[0], spec[1]
    real_taps, real_gated, real_grad = (
        real_spec[..., :width], real_spec[..., width : 2 * width], real_spec[..., 2 * width :]
    )
    imag_taps, imag_gated, imag_grad = (
        imag_spec[..., :width], imag_spec[..., width : 2 * width], imag_spec[..., 2 * width :]
    )
    products = jnp.stack(
        [
            jnp.concatenate(
                [
                    real_taps * real_gated - imag_taps * imag_gated,
                    real_taps * real_grad + imag_taps * imag_grad,
                    real_grad * real_gated + imag_grad * imag_gated,
                ],
                axis=-1,
            ),
            jnp.concatenate(
                [
                    real_taps * imag_gated + imag_taps * real_gated,
                    real_taps * imag_grad - imag_taps * real_grad,
                    imag_grad * real_gated - real_grad * imag_gated,
                ],
                axis=-1,
            ),
        ]
    )
    results = signals(products, tables)
    conv_time = results[:, :width]
    gated_time_back = results[:, width : 2 * width]
    taps_back = results[:, 2 * width :]
    conv = lax.all_to_all(
        conv_time.astype(jnp.bfloat16), "context", split_axis=0, concat_axis=1, tiled=True
    )
    gated_narrow = lax.all_to_all(
        gated_time_back.astype(jnp.bfloat16), "context", split_axis=0, concat_axis=1, tiled=True
    )
    conv_wide = conv.astype(jnp.float32)
    weighted = (query_wide * conv_wide).astype(jnp.bfloat16)
    mixed = blockwise(weighted, output_weight).astype(jnp.bfloat16)
    mixed_rows = lax.all_to_all(mixed, "tensor", split_axis=0, concat_axis=1, tiled=True)
    query_back = (back_weighted * conv_wide).astype(jnp.bfloat16)
    gated_back = gated_narrow.astype(jnp.float32)
    key_back = (gated_back * values.astype(jnp.float32)).astype(jnp.bfloat16)
    value_back = (gated_back * keys.astype(jnp.float32)).astype(jnp.bfloat16)
    token_grad = (
        blockwise_back(query_back, query_weight)
        + blockwise_back(key_back, key_weight)
        + blockwise_back(value_back, value_weight)
    ).astype(jnp.bfloat16)
    factor = 1.0 / math.sqrt(lax.axis_size("dp") * length)
    query_grad, key_grad, value_grad, output_grad = (
        lax.psum(
            (weight_term(inputs, query_back, blocks) * factor).astype(jnp.bfloat16),
            ("dp", "context"),
        ).astype(jnp.float32),
        lax.psum(
            (weight_term(inputs, key_back, blocks) * factor).astype(jnp.bfloat16), ("dp", "context")
        ).astype(jnp.float32),
        lax.psum(
            (weight_term(inputs, value_back, blocks) * factor).astype(jnp.bfloat16),
            ("dp", "context"),
        ).astype(jnp.float32),
        lax.psum(
            (weight_term(weighted, upstream, blocks) * factor).astype(jnp.bfloat16),
            ("dp", "context"),
        ).astype(jnp.float32),
    )
    taps_total = lax.psum((taps_back * factor).astype(jnp.bfloat16), "dp").astype(jnp.float32)
    filter_grad = lax.all_to_all(
        lax.all_to_all(
            taps_total.astype(jnp.bfloat16), "context", split_axis=0, concat_axis=1, tiled=True
        ),
        "tensor",
        split_axis=0,
        concat_axis=1,
        tiled=True,
    ).astype(taps_total.dtype)
    grad_rows = lax.all_to_all(token_grad, "tensor", split_axis=0, concat_axis=1, tiled=True)
    return (
        mixed_rows[None],
        grad_rows[None],
        filter_grad,
        query_grad,
        key_grad,
        value_grad,
        output_grad,
    )


def solution(mesh):
    placed = (
        P("dp", ("context", "tensor"), None),
        P(("context", "tensor"), None),
        P("tensor", None, None),
        P("tensor", None, None),
        P("tensor", None, None),
        P("tensor", None, None),
        P("dp", ("context", "tensor"), None),
    )
    return jax.shard_map(
        shards,
        mesh=mesh,
        in_specs=placed,
        out_specs=(
            P("dp", ("context", "tensor"), None),
            P("dp", ("context", "tensor"), None),
            P(("context", "tensor"), None),
            P("tensor", None, None),
            P("tensor", None, None),
            P("tensor", None, None),
            P("tensor", None, None),
        ),
        check_vma=False,
    )
```

```python
import math

import jax
import jax.numpy as jnp
from jax import lax
from jax.sharding import PartitionSpec as P

table_mode = lax.Precision.HIGH


def blockwise(acts, weight):
    rows = acts.shape[0]
    shaped = acts.reshape(rows, weight.shape[0], weight.shape[1])
    return jnp.einsum("tni,nij->tnj", shaped, weight, preferred_element_type=jnp.float32).reshape(
        rows, -1
    )


def blockwise_back(acts, weight):
    rows = acts.shape[0]
    shaped = acts.reshape(rows, weight.shape[0], weight.shape[1])
    return jnp.einsum("tnj,nij->tni", shaped, weight, preferred_element_type=jnp.float32).reshape(
        rows, -1
    )


def weight_term(inputs, grads, blocks):
    rows = inputs.shape[0]
    left = inputs.reshape(rows, blocks, -1)
    right = grads.reshape(rows, blocks, -1)
    return jnp.einsum("tni,tnj->nij", left, right, preferred_element_type=jnp.float32)


def angle_table(rows, cols, total):
    product = (
        jnp.arange(rows, dtype=jnp.int32)[:, None]
        * jnp.arange(cols, dtype=jnp.int32)[None, :]
        % total
    )
    angle = product.astype(jnp.float32) * (2.0 * math.pi / total)
    return (jnp.cos(angle), jnp.sin(angle))


def make_tables(length):
    second = length // 128
    cosine_first, sine_first = angle_table(128, 128, 128)
    cosine_second, sine_second = angle_table(second, second, second)
    cosine_twist, sine_twist = angle_table(128, second, length)
    return (
        cosine_first,
        sine_first,
        cosine_second,
        sine_second,
        cosine_twist[:, :, None],
        sine_twist[:, :, None],
    )


def across_first(matrix, array):
    return jnp.einsum(
        "kn,nmc->kmc", matrix, array, precision=table_mode, preferred_element_type=jnp.float32
    )


def across_second(array, matrix):
    return jnp.einsum(
        "kmc,ml->klc", array, matrix, precision=table_mode, preferred_element_type=jnp.float32
    )


def forward_transform(signal, tables):
    cosine_first, sine_first, cosine_second, sine_second, cosine_twist, sine_twist = tables
    half = cosine_first.shape[0] // 2
    shaped = signal.reshape(half, cosine_second.shape[0], signal.shape[1])
    real_section = across_first(cosine_first[:, :half], shaped)
    imag_section = -across_first(sine_first[:, :half], shaped)
    real_turned = real_section * cosine_twist + imag_section * sine_twist
    imag_turned = imag_section * cosine_twist - real_section * sine_twist
    real_out = across_second(real_turned, cosine_second) + across_second(imag_turned, sine_second)
    imag_out = across_second(imag_turned, cosine_second) - across_second(real_turned, sine_second)
    return (real_out, imag_out)


def inverse_transform(real_spec, imag_spec, tables):
    cosine_first, sine_first, cosine_second, sine_second, cosine_twist, sine_twist = tables
    half = cosine_first.shape[0] // 2
    total = cosine_first.shape[0] * cosine_second.shape[0]
    real_section = across_second(real_spec, cosine_second) - across_second(imag_spec, sine_second)
    imag_section = across_second(imag_spec, cosine_second) + across_second(real_spec, sine_second)
    real_turned = real_section * cosine_twist - imag_section * sine_twist
    imag_turned = imag_section * cosine_twist + real_section * sine_twist
    signal = (
        across_first(cosine_first[:half], real_turned)
        - across_first(sine_first[:half], imag_turned)
    ) / total
    return signal.reshape(half * cosine_second.shape[0], -1)


def spectral_tables(length):
    first = 128
    second = length // first
    half = first // 2
    cosine_first, sine_first = angle_table(first, first, first)
    cosine_second, sine_second = angle_table(second, second, second)
    cosine_twist, sine_twist = angle_table(first, second, length)
    forward_first = jnp.concatenate([cosine_first[:, :half], -sine_first[:, :half]], axis=0)
    forward_second = jnp.stack(
        [
            jnp.stack([cosine_second, -sine_second], axis=1),
            jnp.stack([sine_second, cosine_second], axis=1),
        ]
    )
    inverse_second = jnp.stack(
        [
            jnp.stack([cosine_second, sine_second], axis=1),
            jnp.stack([-sine_second, cosine_second], axis=1),
        ]
    )
    inverse_first = jnp.stack([cosine_first[:half], -sine_first[:half]], axis=1) / length
    return (
        forward_first,
        forward_second,
        inverse_second,
        inverse_first,
        cosine_twist[:, :, None],
        sine_twist[:, :, None],
    )


def spectra(signal, tables):
    forward_first, forward_second, _, _, cosine_twist, sine_twist = tables
    first = cosine_twist.shape[0]
    half = first // 2
    shaped = signal.reshape(half, cosine_twist.shape[1], signal.shape[1])
    section = jnp.einsum(
        "kn,nmc->kmc", forward_first, shaped, precision=table_mode,
        preferred_element_type=jnp.float32,
    )
    real_section, imag_section = section[:first], section[first:]
    turned = jnp.stack(
        [
            real_section * cosine_twist + imag_section * sine_twist,
            imag_section * cosine_twist - real_section * sine_twist,
        ]
    )
    return jnp.einsum(
        "rkmc,rmsl->sklc", turned, forward_second, precision=table_mode,
        preferred_element_type=jnp.float32,
    )


def signals(spec, tables):
    _, _, inverse_second, inverse_first, cosine_twist, sine_twist = tables
    section = jnp.einsum(
        "sklc,slrm->rkmc", spec, inverse_second, precision=table_mode,
        preferred_element_type=jnp.float32,
    )
    real_section, imag_section = section[0], section[1]
    turned = jnp.stack(
        [
            real_section * cosine_twist - imag_section * sine_twist,
            imag_section * cosine_twist + real_section * sine_twist,
        ]
    )
    out = jnp.einsum(
        "nrk,rkmc->nmc", inverse_first, turned, precision=table_mode,
        preferred_element_type=jnp.float32,
    )
    return out.reshape(-1, out.shape[-1])


def shards(
    tokens, filter_taps, query_weight, key_weight, value_weight, output_weight, out_cotangent
):
    inputs, upstream = (
        lax.all_to_all(tokens[0], "tensor", split_axis=1, concat_axis=0, tiled=True),
        lax.all_to_all(out_cotangent[0], "tensor", split_axis=1, concat_axis=0, tiled=True),
    )
    blocks = query_weight.shape[0]
    query = blockwise(inputs, query_weight).astype(jnp.bfloat16)
    keys = blockwise(inputs, key_weight).astype(jnp.bfloat16)
    values = blockwise(inputs, value_weight).astype(jnp.bfloat16)
    gated = (keys.astype(jnp.float32) * values.astype(jnp.float32)).astype(jnp.bfloat16)
    query_wide = query.astype(jnp.float32)
    taps = lax.all_to_all(
        lax.all_to_all(filter_taps, "tensor", split_axis=1, concat_axis=0, tiled=True),
        "context",
        split_axis=1,
        concat_axis=0,
        tiled=True,
    )
    length = taps.shape[0]
    width = taps.shape[1]
    tables = spectral_tables(2 * length)
    gated_time = lax.all_to_all(gated, "context", split_axis=1, concat_axis=0, tiled=True)
    back_weighted = blockwise_back(upstream, output_weight)
    conv_grad = (back_weighted * query_wide).astype(jnp.bfloat16)
    grad_time = lax.all_to_all(conv_grad, "context", split_axis=1, concat_axis=0, tiled=True)
    spec = spectra(
        jnp.concatenate(
            [taps, gated_time.astype(jnp.float32), grad_time.astype(jnp.float32)], axis=1
        ),
        tables,
    )
    real_spec, imag_spec = spec[0], spec[1]
    real_taps, real_gated, real_grad = (
        real_spec[..., :width], real_spec[..., width : 2 * width], real_spec[..., 2 * width :]
    )
    imag_taps, imag_gated, imag_grad = (
        imag_spec[..., :width], imag_spec[..., width : 2 * width], imag_spec[..., 2 * width :]
    )
    products = jnp.stack(
        [
            jnp.concatenate(
                [
                    real_taps * real_gated - imag_taps * imag_gated,
                    real_taps * real_grad + imag_taps * imag_grad,
                    real_grad * real_gated + imag_grad * imag_gated,
                ],
                axis=-1,
            ),
            jnp.concatenate(
                [
                    real_taps * imag_gated + imag_taps * real_gated,
                    real_taps * imag_grad - imag_taps * real_grad,
                    imag_grad * real_gated - real_grad * imag_gated,
                ],
                axis=-1,
            ),
        ]
    )
    results = signals(products, tables)
    conv_time = results[:, :width]
    gated_time_back = results[:, width : 2 * width]
    taps_back = results[:, 2 * width :]
    conv = lax.all_to_all(
        conv_time.astype(jnp.bfloat16), "context", split_axis=0, concat_axis=1, tiled=True
    )
    gated_narrow = lax.all_to_all(
        gated_time_back.astype(jnp.bfloat16), "context", split_axis=0, concat_axis=1, tiled=True
    )
    conv_wide = conv.astype(jnp.float32)
    weighted = (query_wide * conv_wide).astype(jnp.bfloat16)
    mixed = blockwise(weighted, output_weight).astype(jnp.bfloat16)
    mixed_rows = lax.all_to_all(mixed, "tensor", split_axis=0, concat_axis=1, tiled=True)
    query_back = (back_weighted * conv_wide).astype(jnp.bfloat16)
    gated_back = gated_narrow.astype(jnp.float32)
    key_back = (gated_back * values.astype(jnp.float32)).astype(jnp.bfloat16)
    value_back = (gated_back * keys.astype(jnp.float32)).astype(jnp.bfloat16)
    token_grad = (
        blockwise_back(query_back, query_weight)
        + blockwise_back(key_back, key_weight)
        + blockwise_back(value_back, value_weight)
    ).astype(jnp.bfloat16)
    factor = 1.0 / math.sqrt(lax.axis_size("dp") * length)
    terms = jnp.stack(
        [
            weight_term(inputs, query_back, blocks),
            weight_term(inputs, key_back, blocks),
            weight_term(inputs, value_back, blocks),
            weight_term(weighted, upstream, blocks),
        ]
    )
    group = ("dp", "context")
    members = lax.axis_size("dp") * lax.axis_size("context")
    pieces = lax.all_to_all(
        (terms * factor).astype(jnp.bfloat16).reshape(members, -1),
        group,
        split_axis=0,
        concat_axis=0,
        tiled=True,
    )
    own = jnp.sum(pieces.astype(jnp.float32), axis=0).astype(jnp.bfloat16)
    gathered = lax.all_to_all(
        jnp.broadcast_to(own[None], (members, own.shape[0])),
        group,
        split_axis=0,
        concat_axis=0,
        tiled=True,
    )
    summed = gathered.reshape(terms.shape).astype(jnp.float32)
    query_grad, key_grad, value_grad, output_grad = summed[0], summed[1], summed[2], summed[3]
    taps_total = lax.psum((taps_back * factor).astype(jnp.bfloat16), "dp").astype(jnp.float32)
    filter_grad = lax.all_to_all(
        lax.all_to_all(
            taps_total.astype(jnp.bfloat16), "context", split_axis=0, concat_axis=1, tiled=True
        ),
        "tensor",
        split_axis=0,
        concat_axis=1,
        tiled=True,
    ).astype(taps_total.dtype)
    grad_rows = lax.all_to_all(token_grad, "tensor", split_axis=0, concat_axis=1, tiled=True)
    return (
        mixed_rows[None],
        grad_rows[None],
        filter_grad,
        query_grad,
        key_grad,
        value_grad,
        output_grad,
    )


def solution(mesh):
    placed = (
        P("dp", ("context", "tensor"), None),
        P(("context", "tensor"), None),
        P("tensor", None, None),
        P("tensor", None, None),
        P("tensor", None, None),
        P("tensor", None, None),
        P("dp", ("context", "tensor"), None),
    )
    return jax.shard_map(
        shards,
        mesh=mesh,
        in_specs=placed,
        out_specs=(
            P("dp", ("context", "tensor"), None),
            P("dp", ("context", "tensor"), None),
            P(("context", "tensor"), None),
            P("tensor", None, None),
            P("tensor", None, None),
            P("tensor", None, None),
            P("tensor", None, None),
        ),
        check_vma=False,
    )
```

```python
import math

import jax
import jax.numpy as jnp
from jax import lax
from jax.sharding import PartitionSpec as P

table_mode = lax.Precision.DEFAULT


def blockwise(acts, weight):
    rows = acts.shape[0]
    shaped = acts.reshape(rows, weight.shape[0], weight.shape[1])
    return jnp.einsum("tni,nij->tnj", shaped, weight, preferred_element_type=jnp.float32).reshape(
        rows, -1
    )


def blockwise_back(acts, weight):
    rows = acts.shape[0]
    shaped = acts.reshape(rows, weight.shape[0], weight.shape[1])
    return jnp.einsum("tnj,nij->tni", shaped, weight, preferred_element_type=jnp.float32).reshape(
        rows, -1
    )


def weight_term(inputs, grads, blocks):
    rows = inputs.shape[0]
    left = inputs.reshape(rows, blocks, -1)
    right = grads.reshape(rows, blocks, -1)
    return jnp.einsum("tni,tnj->nij", left, right, preferred_element_type=jnp.float32)


def angle_table(rows, cols, total):
    product = (
        jnp.arange(rows, dtype=jnp.int32)[:, None]
        * jnp.arange(cols, dtype=jnp.int32)[None, :]
        % total
    )
    angle = product.astype(jnp.float32) * (2.0 * math.pi / total)
    return (jnp.cos(angle), jnp.sin(angle))


def make_tables(length):
    second = length // 128
    cosine_first, sine_first = angle_table(128, 128, 128)
    cosine_second, sine_second = angle_table(second, second, second)
    cosine_twist, sine_twist = angle_table(128, second, length)
    return (
        cosine_first,
        sine_first,
        cosine_second,
        sine_second,
        cosine_twist[:, :, None],
        sine_twist[:, :, None],
    )


def across_first(matrix, array):
    return jnp.einsum(
        "kn,nmc->kmc", matrix, array, precision=table_mode, preferred_element_type=jnp.float32
    )


def across_second(array, matrix):
    return jnp.einsum(
        "kmc,ml->klc", array, matrix, precision=table_mode, preferred_element_type=jnp.float32
    )


def forward_transform(signal, tables):
    cosine_first, sine_first, cosine_second, sine_second, cosine_twist, sine_twist = tables
    half = cosine_first.shape[0] // 2
    shaped = signal.reshape(half, cosine_second.shape[0], signal.shape[1])
    real_section = across_first(cosine_first[:, :half], shaped)
    imag_section = -across_first(sine_first[:, :half], shaped)
    real_turned = real_section * cosine_twist + imag_section * sine_twist
    imag_turned = imag_section * cosine_twist - real_section * sine_twist
    real_out = across_second(real_turned, cosine_second) + across_second(imag_turned, sine_second)
    imag_out = across_second(imag_turned, cosine_second) - across_second(real_turned, sine_second)
    return (real_out, imag_out)


def inverse_transform(real_spec, imag_spec, tables):
    cosine_first, sine_first, cosine_second, sine_second, cosine_twist, sine_twist = tables
    half = cosine_first.shape[0] // 2
    total = cosine_first.shape[0] * cosine_second.shape[0]
    real_section = across_second(real_spec, cosine_second) - across_second(imag_spec, sine_second)
    imag_section = across_second(imag_spec, cosine_second) + across_second(real_spec, sine_second)
    real_turned = real_section * cosine_twist - imag_section * sine_twist
    imag_turned = imag_section * cosine_twist + real_section * sine_twist
    signal = (
        across_first(cosine_first[:half], real_turned)
        - across_first(sine_first[:half], imag_turned)
    ) / total
    return signal.reshape(half * cosine_second.shape[0], -1)


def spectral_tables(length):
    first = 128
    second = length // first
    half = first // 2
    cosine_first, sine_first = angle_table(first, first, first)
    cosine_second, sine_second = angle_table(second, second, second)
    cosine_twist, sine_twist = angle_table(first, second, length)
    forward_first = jnp.concatenate([cosine_first[:, :half], -sine_first[:, :half]], axis=0)
    forward_second = jnp.stack(
        [
            jnp.stack([cosine_second, -sine_second], axis=1),
            jnp.stack([sine_second, cosine_second], axis=1),
        ]
    )
    inverse_second = jnp.stack(
        [
            jnp.stack([cosine_second, sine_second], axis=1),
            jnp.stack([-sine_second, cosine_second], axis=1),
        ]
    )
    inverse_first = jnp.stack([cosine_first[:half], -sine_first[:half]], axis=1) / length
    return (
        forward_first,
        forward_second,
        inverse_second,
        inverse_first,
        cosine_twist[:, :, None],
        sine_twist[:, :, None],
    )


def spectra(signal, tables):
    forward_first, forward_second, _, _, cosine_twist, sine_twist = tables
    first = cosine_twist.shape[0]
    half = first // 2
    shaped = signal.reshape(half, cosine_twist.shape[1], signal.shape[1])
    section = jnp.einsum(
        "kn,nmc->kmc", forward_first, shaped, precision=table_mode,
        preferred_element_type=jnp.float32,
    )
    real_section, imag_section = section[:first], section[first:]
    turned = jnp.stack(
        [
            real_section * cosine_twist + imag_section * sine_twist,
            imag_section * cosine_twist - real_section * sine_twist,
        ]
    )
    return jnp.einsum(
        "rkmc,rmsl->sklc", turned, forward_second, precision=table_mode,
        preferred_element_type=jnp.float32,
    )


def signals(spec, tables):
    _, _, inverse_second, inverse_first, cosine_twist, sine_twist = tables
    section = jnp.einsum(
        "sklc,slrm->rkmc", spec, inverse_second, precision=table_mode,
        preferred_element_type=jnp.float32,
    )
    real_section, imag_section = section[0], section[1]
    turned = jnp.stack(
        [
            real_section * cosine_twist - imag_section * sine_twist,
            imag_section * cosine_twist + real_section * sine_twist,
        ]
    )
    out = jnp.einsum(
        "nrk,rkmc->nmc", inverse_first, turned, precision=table_mode,
        preferred_element_type=jnp.float32,
    )
    return out.reshape(-1, out.shape[-1])


def shards(
    tokens, filter_taps, query_weight, key_weight, value_weight, output_weight, out_cotangent
):
    inputs, upstream = (
        lax.all_to_all(tokens[0], "tensor", split_axis=1, concat_axis=0, tiled=True),
        lax.all_to_all(out_cotangent[0], "tensor", split_axis=1, concat_axis=0, tiled=True),
    )
    blocks = query_weight.shape[0]
    query = blockwise(inputs, query_weight).astype(jnp.bfloat16)
    keys = blockwise(inputs, key_weight).astype(jnp.bfloat16)
    values = blockwise(inputs, value_weight).astype(jnp.bfloat16)
    gated = (keys.astype(jnp.float32) * values.astype(jnp.float32)).astype(jnp.bfloat16)
    query_wide = query.astype(jnp.float32)
    taps = lax.all_to_all(
        lax.all_to_all(filter_taps, "tensor", split_axis=1, concat_axis=0, tiled=True),
        "context",
        split_axis=1,
        concat_axis=0,
        tiled=True,
    )
    length = taps.shape[0]
    width = taps.shape[1]
    tables = spectral_tables(2 * length)
    gated_time = lax.all_to_all(gated, "context", split_axis=1, concat_axis=0, tiled=True)
    back_weighted = blockwise_back(upstream, output_weight)
    conv_grad = (back_weighted * query_wide).astype(jnp.bfloat16)
    grad_time = lax.all_to_all(conv_grad, "context", split_axis=1, concat_axis=0, tiled=True)
    spec = spectra(
        jnp.concatenate(
            [taps, gated_time.astype(jnp.float32), grad_time.astype(jnp.float32)], axis=1
        ),
        tables,
    )
    real_spec, imag_spec = spec[0], spec[1]
    real_taps, real_gated, real_grad = (
        real_spec[..., :width], real_spec[..., width : 2 * width], real_spec[..., 2 * width :]
    )
    imag_taps, imag_gated, imag_grad = (
        imag_spec[..., :width], imag_spec[..., width : 2 * width], imag_spec[..., 2 * width :]
    )
    products = jnp.stack(
        [
            jnp.concatenate(
                [
                    real_taps * real_gated - imag_taps * imag_gated,
                    real_taps * real_grad + imag_taps * imag_grad,
                    real_grad * real_gated + imag_grad * imag_gated,
                ],
                axis=-1,
            ),
            jnp.concatenate(
                [
                    real_taps * imag_gated + imag_taps * real_gated,
                    real_taps * imag_grad - imag_taps * real_grad,
                    imag_grad * real_gated - real_grad * imag_gated,
                ],
                axis=-1,
            ),
        ]
    )
    results = signals(products, tables)
    conv_time = results[:, :width]
    gated_time_back = results[:, width : 2 * width]
    taps_back = results[:, 2 * width :]
    conv = lax.all_to_all(
        conv_time.astype(jnp.bfloat16), "context", split_axis=0, concat_axis=1, tiled=True
    )
    gated_narrow = lax.all_to_all(
        gated_time_back.astype(jnp.bfloat16), "context", split_axis=0, concat_axis=1, tiled=True
    )
    conv_wide = conv.astype(jnp.float32)
    weighted = (query_wide * conv_wide).astype(jnp.bfloat16)
    mixed = blockwise(weighted, output_weight).astype(jnp.bfloat16)
    mixed_rows = lax.all_to_all(mixed, "tensor", split_axis=0, concat_axis=1, tiled=True)
    query_back = (back_weighted * conv_wide).astype(jnp.bfloat16)
    gated_back = gated_narrow.astype(jnp.float32)
    key_back = (gated_back * values.astype(jnp.float32)).astype(jnp.bfloat16)
    value_back = (gated_back * keys.astype(jnp.float32)).astype(jnp.bfloat16)
    token_grad = (
        blockwise_back(query_back, query_weight)
        + blockwise_back(key_back, key_weight)
        + blockwise_back(value_back, value_weight)
    ).astype(jnp.bfloat16)
    factor = 1.0 / math.sqrt(lax.axis_size("dp") * length)
    query_grad, key_grad, value_grad, output_grad = (
        lax.psum(
            (weight_term(inputs, query_back, blocks) * factor).astype(jnp.bfloat16),
            ("dp", "context"),
        ).astype(jnp.float32),
        lax.psum(
            (weight_term(inputs, key_back, blocks) * factor).astype(jnp.bfloat16), ("dp", "context")
        ).astype(jnp.float32),
        lax.psum(
            (weight_term(inputs, value_back, blocks) * factor).astype(jnp.bfloat16),
            ("dp", "context"),
        ).astype(jnp.float32),
        lax.psum(
            (weight_term(weighted, upstream, blocks) * factor).astype(jnp.bfloat16),
            ("dp", "context"),
        ).astype(jnp.float32),
    )
    taps_total = lax.psum((taps_back * factor).astype(jnp.bfloat16), "dp").astype(jnp.float32)
    filter_grad = lax.all_to_all(
        lax.all_to_all(
            taps_total.astype(jnp.bfloat16), "context", split_axis=0, concat_axis=1, tiled=True
        ),
        "tensor",
        split_axis=0,
        concat_axis=1,
        tiled=True,
    ).astype(taps_total.dtype)
    grad_rows = lax.all_to_all(token_grad, "tensor", split_axis=0, concat_axis=1, tiled=True)
    return (
        mixed_rows[None],
        grad_rows[None],
        filter_grad,
        query_grad,
        key_grad,
        value_grad,
        output_grad,
    )


def solution(mesh):
    placed = (
        P("dp", ("context", "tensor"), None),
        P(("context", "tensor"), None),
        P("tensor", None, None),
        P("tensor", None, None),
        P("tensor", None, None),
        P("tensor", None, None),
        P("dp", ("context", "tensor"), None),
    )
    return jax.shard_map(
        shards,
        mesh=mesh,
        in_specs=placed,
        out_specs=(
            P("dp", ("context", "tensor"), None),
            P("dp", ("context", "tensor"), None),
            P(("context", "tensor"), None),
            P("tensor", None, None),
            P("tensor", None, None),
            P("tensor", None, None),
            P("tensor", None, None),
        ),
        check_vma=False,
    )
```

```python
import math

import jax
import jax.numpy as jnp
from jax import lax
from jax.sharding import PartitionSpec as P

table_mode = lax.Precision.DEFAULT


def blockwise(acts, weight):
    rows = acts.shape[0]
    shaped = acts.reshape(rows, weight.shape[0], weight.shape[1])
    return jnp.einsum("tni,nij->tnj", shaped, weight, preferred_element_type=jnp.float32).reshape(
        rows, -1
    )


def blockwise_back(acts, weight):
    rows = acts.shape[0]
    shaped = acts.reshape(rows, weight.shape[0], weight.shape[1])
    return jnp.einsum("tnj,nij->tni", shaped, weight, preferred_element_type=jnp.float32).reshape(
        rows, -1
    )


def weight_term(inputs, grads, blocks):
    rows = inputs.shape[0]
    left = inputs.reshape(rows, blocks, -1)
    right = grads.reshape(rows, blocks, -1)
    return jnp.einsum("tni,tnj->nij", left, right, preferred_element_type=jnp.float32)


def angle_table(rows, cols, total):
    product = (
        jnp.arange(rows, dtype=jnp.int32)[:, None]
        * jnp.arange(cols, dtype=jnp.int32)[None, :]
        % total
    )
    angle = product.astype(jnp.float32) * (2.0 * math.pi / total)
    return (jnp.cos(angle), jnp.sin(angle))


def make_tables(length):
    second = length // 128
    cosine_first, sine_first = angle_table(128, 128, 128)
    cosine_second, sine_second = angle_table(second, second, second)
    cosine_twist, sine_twist = angle_table(128, second, length)
    return (
        cosine_first,
        sine_first,
        cosine_second,
        sine_second,
        cosine_twist[:, :, None],
        sine_twist[:, :, None],
    )


def across_first(matrix, array):
    return jnp.einsum(
        "kn,nmc->kmc", matrix, array, precision=table_mode, preferred_element_type=jnp.float32
    )


def across_second(array, matrix):
    return jnp.einsum(
        "kmc,ml->klc", array, matrix, precision=table_mode, preferred_element_type=jnp.float32
    )


def forward_transform(signal, tables):
    cosine_first, sine_first, cosine_second, sine_second, cosine_twist, sine_twist = tables
    half = cosine_first.shape[0] // 2
    shaped = signal.reshape(half, cosine_second.shape[0], signal.shape[1])
    real_section = across_first(cosine_first[:, :half], shaped)
    imag_section = -across_first(sine_first[:, :half], shaped)
    real_turned = real_section * cosine_twist + imag_section * sine_twist
    imag_turned = imag_section * cosine_twist - real_section * sine_twist
    real_out = across_second(real_turned, cosine_second) + across_second(imag_turned, sine_second)
    imag_out = across_second(imag_turned, cosine_second) - across_second(real_turned, sine_second)
    return (real_out, imag_out)


def inverse_transform(real_spec, imag_spec, tables):
    cosine_first, sine_first, cosine_second, sine_second, cosine_twist, sine_twist = tables
    half = cosine_first.shape[0] // 2
    total = cosine_first.shape[0] * cosine_second.shape[0]
    real_section = across_second(real_spec, cosine_second) - across_second(imag_spec, sine_second)
    imag_section = across_second(imag_spec, cosine_second) + across_second(real_spec, sine_second)
    real_turned = real_section * cosine_twist - imag_section * sine_twist
    imag_turned = imag_section * cosine_twist + real_section * sine_twist
    signal = (
        across_first(cosine_first[:half], real_turned)
        - across_first(sine_first[:half], imag_turned)
    ) / total
    return signal.reshape(half * cosine_second.shape[0], -1)


def spectral_tables(length):
    first = 128
    second = length // first
    half = first // 2
    cosine_first, sine_first = angle_table(first, first, first)
    cosine_second, sine_second = angle_table(second, second, second)
    cosine_twist, sine_twist = angle_table(first, second, length)
    forward_first = jnp.concatenate([cosine_first[:, :half], -sine_first[:, :half]], axis=0)
    forward_second = jnp.stack(
        [
            jnp.stack([cosine_second, -sine_second], axis=1),
            jnp.stack([sine_second, cosine_second], axis=1),
        ]
    )
    inverse_second = jnp.stack(
        [
            jnp.stack([cosine_second, sine_second], axis=1),
            jnp.stack([-sine_second, cosine_second], axis=1),
        ]
    )
    inverse_first = jnp.stack([cosine_first[:half], -sine_first[:half]], axis=1) / length
    return (
        forward_first,
        forward_second,
        inverse_second,
        inverse_first,
        cosine_twist[:, :, None],
        sine_twist[:, :, None],
    )


def spectra(signal, tables):
    forward_first, forward_second, _, _, cosine_twist, sine_twist = tables
    first = cosine_twist.shape[0]
    half = first // 2
    shaped = signal.reshape(half, cosine_twist.shape[1], signal.shape[1])
    section = jnp.einsum(
        "kn,nmc->kmc", forward_first, shaped, precision=table_mode,
        preferred_element_type=jnp.float32,
    )
    real_section, imag_section = section[:first], section[first:]
    turned = jnp.stack(
        [
            real_section * cosine_twist + imag_section * sine_twist,
            imag_section * cosine_twist - real_section * sine_twist,
        ]
    )
    return jnp.einsum(
        "rkmc,rmsl->sklc", turned, forward_second, precision=table_mode,
        preferred_element_type=jnp.float32,
    )


def signals(spec, tables):
    _, _, inverse_second, inverse_first, cosine_twist, sine_twist = tables
    section = jnp.einsum(
        "sklc,slrm->rkmc", spec, inverse_second, precision=table_mode,
        preferred_element_type=jnp.float32,
    )
    real_section, imag_section = section[0], section[1]
    turned = jnp.stack(
        [
            real_section * cosine_twist - imag_section * sine_twist,
            imag_section * cosine_twist + real_section * sine_twist,
        ]
    )
    out = jnp.einsum(
        "nrk,rkmc->nmc", inverse_first, turned, precision=table_mode,
        preferred_element_type=jnp.float32,
    )
    return out.reshape(-1, out.shape[-1])


def shards(
    tokens, filter_taps, query_weight, key_weight, value_weight, output_weight, out_cotangent
):
    inputs, upstream = (
        lax.all_to_all(tokens[0], "tensor", split_axis=1, concat_axis=0, tiled=True),
        lax.all_to_all(out_cotangent[0], "tensor", split_axis=1, concat_axis=0, tiled=True),
    )
    blocks = query_weight.shape[0]
    query = blockwise(inputs, query_weight).astype(jnp.bfloat16)
    keys = blockwise(inputs, key_weight).astype(jnp.bfloat16)
    values = blockwise(inputs, value_weight).astype(jnp.bfloat16)
    gated = (keys.astype(jnp.float32) * values.astype(jnp.float32)).astype(jnp.bfloat16)
    query_wide = query.astype(jnp.float32)
    taps = lax.all_to_all(
        lax.all_to_all(filter_taps, "tensor", split_axis=1, concat_axis=0, tiled=True),
        "context",
        split_axis=1,
        concat_axis=0,
        tiled=True,
    )
    length = taps.shape[0]
    width = taps.shape[1]
    tables = spectral_tables(2 * length)
    gated_time = lax.all_to_all(gated, "context", split_axis=1, concat_axis=0, tiled=True)
    back_weighted = blockwise_back(upstream, output_weight)
    conv_grad = (back_weighted * query_wide).astype(jnp.bfloat16)
    grad_time = lax.all_to_all(conv_grad, "context", split_axis=1, concat_axis=0, tiled=True)
    spec = spectra(
        jnp.concatenate(
            [taps, gated_time.astype(jnp.float32), grad_time.astype(jnp.float32)], axis=1
        ),
        tables,
    )
    real_spec, imag_spec = spec[0], spec[1]
    real_taps, real_gated, real_grad = (
        real_spec[..., :width], real_spec[..., width : 2 * width], real_spec[..., 2 * width :]
    )
    imag_taps, imag_gated, imag_grad = (
        imag_spec[..., :width], imag_spec[..., width : 2 * width], imag_spec[..., 2 * width :]
    )
    products = jnp.stack(
        [
            jnp.concatenate(
                [
                    real_taps * real_gated - imag_taps * imag_gated,
                    real_taps * real_grad + imag_taps * imag_grad,
                    real_grad * real_gated + imag_grad * imag_gated,
                ],
                axis=-1,
            ),
            jnp.concatenate(
                [
                    real_taps * imag_gated + imag_taps * real_gated,
                    real_taps * imag_grad - imag_taps * real_grad,
                    imag_grad * real_gated - real_grad * imag_gated,
                ],
                axis=-1,
            ),
        ]
    )
    results = signals(products, tables)
    conv_time = results[:, :width]
    gated_time_back = results[:, width : 2 * width]
    taps_back = results[:, 2 * width :]
    conv = lax.all_to_all(
        conv_time.astype(jnp.bfloat16), "context", split_axis=0, concat_axis=1, tiled=True
    )
    gated_narrow = lax.all_to_all(
        gated_time_back.astype(jnp.bfloat16), "context", split_axis=0, concat_axis=1, tiled=True
    )
    conv_wide = conv.astype(jnp.float32)
    weighted = (query_wide * conv_wide).astype(jnp.bfloat16)
    query_back = (back_weighted * conv_wide).astype(jnp.bfloat16)
    gated_back = gated_narrow.astype(jnp.float32)
    key_back = (gated_back * values.astype(jnp.float32)).astype(jnp.bfloat16)
    value_back = (gated_back * keys.astype(jnp.float32)).astype(jnp.bfloat16)
    factor = 1.0 / math.sqrt(lax.axis_size("dp") * length)
    terms = (
        (weight_term(inputs, query_back, blocks) * factor).astype(jnp.bfloat16),
        (weight_term(inputs, key_back, blocks) * factor).astype(jnp.bfloat16),
        (weight_term(inputs, value_back, blocks) * factor).astype(jnp.bfloat16),
        (weight_term(weighted, upstream, blocks) * factor).astype(jnp.bfloat16),
    )
    terms, (query_back, key_back, value_back, weighted) = lax.optimization_barrier(
        (terms, (query_back, key_back, value_back, weighted))
    )
    query_grad, key_grad, value_grad, output_grad = (
        lax.psum(term, ("dp", "context")).astype(jnp.float32) for term in terms
    )
    mixed = blockwise(weighted, output_weight).astype(jnp.bfloat16)
    mixed_rows = lax.all_to_all(mixed, "tensor", split_axis=0, concat_axis=1, tiled=True)
    token_grad = (
        blockwise_back(query_back, query_weight)
        + blockwise_back(key_back, key_weight)
        + blockwise_back(value_back, value_weight)
    ).astype(jnp.bfloat16)
    taps_total = lax.psum((taps_back * factor).astype(jnp.bfloat16), "dp").astype(jnp.float32)
    filter_grad = lax.all_to_all(
        lax.all_to_all(
            taps_total.astype(jnp.bfloat16), "context", split_axis=0, concat_axis=1, tiled=True
        ),
        "tensor",
        split_axis=0,
        concat_axis=1,
        tiled=True,
    ).astype(taps_total.dtype)
    grad_rows = lax.all_to_all(token_grad, "tensor", split_axis=0, concat_axis=1, tiled=True)
    return (
        mixed_rows[None],
        grad_rows[None],
        filter_grad,
        query_grad,
        key_grad,
        value_grad,
        output_grad,
    )


def solution(mesh):
    placed = (
        P("dp", ("context", "tensor"), None),
        P(("context", "tensor"), None),
        P("tensor", None, None),
        P("tensor", None, None),
        P("tensor", None, None),
        P("tensor", None, None),
        P("dp", ("context", "tensor"), None),
    )
    return jax.shard_map(
        shards,
        mesh=mesh,
        in_specs=placed,
        out_specs=(
            P("dp", ("context", "tensor"), None),
            P("dp", ("context", "tensor"), None),
            P(("context", "tensor"), None),
            P("tensor", None, None),
            P("tensor", None, None),
            P("tensor", None, None),
            P("tensor", None, None),
        ),
        check_vma=False,
    )
```

```python
import math

import jax
import jax.numpy as jnp
from jax import lax
from jax.sharding import PartitionSpec as P

table_mode = lax.Precision.DEFAULT


def blockwise(acts, weight):
    rows = acts.shape[0]
    shaped = acts.reshape(rows, weight.shape[0], weight.shape[1])
    return jnp.einsum("tni,nij->tnj", shaped, weight, preferred_element_type=jnp.float32).reshape(
        rows, -1
    )


def blockwise_back(acts, weight):
    rows = acts.shape[0]
    shaped = acts.reshape(rows, weight.shape[0], weight.shape[1])
    return jnp.einsum("tnj,nij->tni", shaped, weight, preferred_element_type=jnp.float32).reshape(
        rows, -1
    )


def weight_term(inputs, grads, blocks):
    rows = inputs.shape[0]
    left = inputs.reshape(rows, blocks, -1)
    right = grads.reshape(rows, blocks, -1)
    return jnp.einsum("tni,tnj->nij", left, right, preferred_element_type=jnp.float32)


def angle_table(rows, cols, total):
    product = (
        jnp.arange(rows, dtype=jnp.int32)[:, None]
        * jnp.arange(cols, dtype=jnp.int32)[None, :]
        % total
    )
    angle = product.astype(jnp.float32) * (2.0 * math.pi / total)
    return (jnp.cos(angle), jnp.sin(angle))


def make_tables(length):
    second = length // 128
    cosine_first, sine_first = angle_table(128, 128, 128)
    cosine_second, sine_second = angle_table(second, second, second)
    cosine_twist, sine_twist = angle_table(128, second, length)
    return (
        cosine_first,
        sine_first,
        cosine_second,
        sine_second,
        cosine_twist[:, :, None],
        sine_twist[:, :, None],
    )


def across_first(matrix, array):
    return jnp.einsum(
        "kn,nmc->kmc", matrix, array, precision=table_mode, preferred_element_type=jnp.float32
    )


def across_second(array, matrix):
    return jnp.einsum(
        "kmc,ml->klc", array, matrix, precision=table_mode, preferred_element_type=jnp.float32
    )


def forward_transform(signal, tables):
    cosine_first, sine_first, cosine_second, sine_second, cosine_twist, sine_twist = tables
    half = cosine_first.shape[0] // 2
    shaped = signal.reshape(half, cosine_second.shape[0], signal.shape[1])
    real_section = across_first(cosine_first[:, :half], shaped)
    imag_section = -across_first(sine_first[:, :half], shaped)
    real_turned = real_section * cosine_twist + imag_section * sine_twist
    imag_turned = imag_section * cosine_twist - real_section * sine_twist
    real_out = across_second(real_turned, cosine_second) + across_second(imag_turned, sine_second)
    imag_out = across_second(imag_turned, cosine_second) - across_second(real_turned, sine_second)
    return (real_out, imag_out)


def inverse_transform(real_spec, imag_spec, tables):
    cosine_first, sine_first, cosine_second, sine_second, cosine_twist, sine_twist = tables
    half = cosine_first.shape[0] // 2
    total = cosine_first.shape[0] * cosine_second.shape[0]
    real_section = across_second(real_spec, cosine_second) - across_second(imag_spec, sine_second)
    imag_section = across_second(imag_spec, cosine_second) + across_second(real_spec, sine_second)
    real_turned = real_section * cosine_twist - imag_section * sine_twist
    imag_turned = imag_section * cosine_twist + real_section * sine_twist
    signal = (
        across_first(cosine_first[:half], real_turned)
        - across_first(sine_first[:half], imag_turned)
    ) / total
    return signal.reshape(half * cosine_second.shape[0], -1)


def spectral_tables(length):
    first = 128
    second = length // first
    half = first // 2
    cosine_first, sine_first = angle_table(first, first, first)
    cosine_second, sine_second = angle_table(second, second, second)
    cosine_twist, sine_twist = angle_table(first, second, length)
    forward_first = jnp.concatenate([cosine_first[:, :half], -sine_first[:, :half]], axis=0)
    forward_second = jnp.stack(
        [
            jnp.stack([cosine_second, -sine_second], axis=1),
            jnp.stack([sine_second, cosine_second], axis=1),
        ]
    )
    inverse_second = jnp.stack(
        [
            jnp.stack([cosine_second, sine_second], axis=1),
            jnp.stack([-sine_second, cosine_second], axis=1),
        ]
    )
    inverse_first = jnp.stack([cosine_first[:half], -sine_first[:half]], axis=1) / length
    return (
        forward_first,
        forward_second,
        inverse_second,
        inverse_first,
        cosine_twist[:, :, None],
        sine_twist[:, :, None],
    )


def spectra(signal, tables):
    forward_first, forward_second, _, _, cosine_twist, sine_twist = tables
    first = cosine_twist.shape[0]
    half = first // 2
    shaped = signal.reshape(half, cosine_twist.shape[1], signal.shape[1])
    section = jnp.einsum(
        "kn,nmc->kmc", forward_first, shaped, precision=table_mode,
        preferred_element_type=jnp.float32,
    )
    real_section, imag_section = section[:first], section[first:]
    turned = jnp.stack(
        [
            real_section * cosine_twist + imag_section * sine_twist,
            imag_section * cosine_twist - real_section * sine_twist,
        ]
    )
    return jnp.einsum(
        "rkmc,rmsl->sklc", turned, forward_second, precision=table_mode,
        preferred_element_type=jnp.float32,
    )


def signals(spec, tables):
    _, _, inverse_second, inverse_first, cosine_twist, sine_twist = tables
    section = jnp.einsum(
        "sklc,slrm->rkmc", spec, inverse_second, precision=table_mode,
        preferred_element_type=jnp.float32,
    )
    real_section, imag_section = section[0], section[1]
    turned = jnp.stack(
        [
            real_section * cosine_twist - imag_section * sine_twist,
            imag_section * cosine_twist + real_section * sine_twist,
        ]
    )
    out = jnp.einsum(
        "nrk,rkmc->nmc", inverse_first, turned, precision=table_mode,
        preferred_element_type=jnp.float32,
    )
    return out.reshape(-1, out.shape[-1])


def shards(
    tokens, filter_taps, query_weight, key_weight, value_weight, output_weight, out_cotangent
):
    ctx = lax.axis_size("context")
    ten = lax.axis_size("tensor")
    rows = tokens.shape[1]
    arrived = lax.all_to_all(
        jnp.concatenate(
            [tokens[0], out_cotangent[0], filter_taps.astype(jnp.bfloat16)], axis=0
        ),
        "tensor",
        split_axis=1,
        concat_axis=0,
        tiled=True,
    )
    arrived = arrived.reshape(ten, 3, rows, arrived.shape[1])
    inputs = arrived[:, 0].reshape(ten * rows, -1)
    upstream = arrived[:, 1].reshape(ten * rows, -1)
    taps_mid = arrived[:, 2].reshape(ten * rows, -1)
    blocks = query_weight.shape[0]
    query = blockwise(inputs, query_weight).astype(jnp.bfloat16)
    keys = blockwise(inputs, key_weight).astype(jnp.bfloat16)
    values = blockwise(inputs, value_weight).astype(jnp.bfloat16)
    gated = (keys.astype(jnp.float32) * values.astype(jnp.float32)).astype(jnp.bfloat16)
    query_wide = query.astype(jnp.float32)
    back_weighted = blockwise_back(upstream, output_weight)
    conv_grad = (back_weighted * query_wide).astype(jnp.bfloat16)
    local = inputs.shape[0]
    timed = lax.all_to_all(
        jnp.concatenate([gated, conv_grad, taps_mid], axis=0),
        "context",
        split_axis=1,
        concat_axis=0,
        tiled=True,
    )
    timed = timed.reshape(ctx, 3, local, timed.shape[1])
    gated_time = timed[:, 0].reshape(ctx * local, -1)
    grad_time = timed[:, 1].reshape(ctx * local, -1)
    taps = timed[:, 2].reshape(ctx * local, -1).astype(jnp.float32)
    length = taps.shape[0]
    width = taps.shape[1]
    tables = spectral_tables(2 * length)
    spec = spectra(
        jnp.concatenate(
            [taps, gated_time.astype(jnp.float32), grad_time.astype(jnp.float32)], axis=1
        ),
        tables,
    )
    real_spec, imag_spec = spec[0], spec[1]
    real_taps, real_gated, real_grad = (
        real_spec[..., :width], real_spec[..., width : 2 * width], real_spec[..., 2 * width :]
    )
    imag_taps, imag_gated, imag_grad = (
        imag_spec[..., :width], imag_spec[..., width : 2 * width], imag_spec[..., 2 * width :]
    )
    products = jnp.stack(
        [
            jnp.concatenate(
                [
                    real_taps * real_gated - imag_taps * imag_gated,
                    real_taps * real_grad + imag_taps * imag_grad,
                    real_grad * real_gated + imag_grad * imag_gated,
                ],
                axis=-1,
            ),
            jnp.concatenate(
                [
                    real_taps * imag_gated + imag_taps * real_gated,
                    real_taps * imag_grad - imag_taps * real_grad,
                    imag_grad * real_gated - real_grad * imag_gated,
                ],
                axis=-1,
            ),
        ]
    )
    results = signals(products, tables)
    conv_time = results[:, :width]
    gated_time_back = results[:, width : 2 * width]
    taps_back = results[:, 2 * width :]
    returned = lax.all_to_all(
        jnp.stack(
            [
                conv_time.astype(jnp.bfloat16).reshape(ctx, local, width),
                gated_time_back.astype(jnp.bfloat16).reshape(ctx, local, width),
            ],
            axis=1,
        ).reshape(ctx * 2 * local, width),
        "context",
        split_axis=0,
        concat_axis=1,
        tiled=True,
    )
    conv, gated_narrow = returned[:local], returned[local:]
    conv_wide = conv.astype(jnp.float32)
    weighted = (query_wide * conv_wide).astype(jnp.bfloat16)
    query_back = (back_weighted * conv_wide).astype(jnp.bfloat16)
    gated_back = gated_narrow.astype(jnp.float32)
    key_back = (gated_back * values.astype(jnp.float32)).astype(jnp.bfloat16)
    value_back = (gated_back * keys.astype(jnp.float32)).astype(jnp.bfloat16)
    factor = 1.0 / math.sqrt(lax.axis_size("dp") * length)
    terms = (
        (weight_term(inputs, query_back, blocks) * factor).astype(jnp.bfloat16),
        (weight_term(inputs, key_back, blocks) * factor).astype(jnp.bfloat16),
        (weight_term(inputs, value_back, blocks) * factor).astype(jnp.bfloat16),
        (weight_term(weighted, upstream, blocks) * factor).astype(jnp.bfloat16),
    )
    terms, (query_back, key_back, value_back, weighted) = lax.optimization_barrier(
        (terms, (query_back, key_back, value_back, weighted))
    )
    query_grad, key_grad, value_grad, output_grad = (
        lax.psum(term, ("dp", "context")).astype(jnp.float32) for term in terms
    )
    mixed = blockwise(weighted, output_weight).astype(jnp.bfloat16)
    token_grad = (
        blockwise_back(query_back, query_weight)
        + blockwise_back(key_back, key_weight)
        + blockwise_back(value_back, value_weight)
    ).astype(jnp.bfloat16)
    taps_total = lax.psum((taps_back * factor).astype(jnp.bfloat16), "dp")
    filter_mid = lax.all_to_all(taps_total, "context", split_axis=0, concat_axis=1, tiled=True)
    leaving = lax.all_to_all(
        jnp.stack(
            [
                part.reshape(ten, rows, part.shape[1])
                for part in (mixed, token_grad, filter_mid)
            ],
            axis=1,
        ).reshape(ten * 3 * rows, -1),
        "tensor",
        split_axis=0,
        concat_axis=1,
        tiled=True,
    )
    mixed_rows = leaving[:rows]
    grad_rows = leaving[rows : 2 * rows]
    filter_grad = leaving[2 * rows :].astype(jnp.float32)
    return (
        mixed_rows[None],
        grad_rows[None],
        filter_grad,
        query_grad,
        key_grad,
        value_grad,
        output_grad,
    )


def solution(mesh):
    placed = (
        P("dp", ("context", "tensor"), None),
        P(("context", "tensor"), None),
        P("tensor", None, None),
        P("tensor", None, None),
        P("tensor", None, None),
        P("tensor", None, None),
        P("dp", ("context", "tensor"), None),
    )
    return jax.shard_map(
        shards,
        mesh=mesh,
        in_specs=placed,
        out_specs=(
            P("dp", ("context", "tensor"), None),
            P("dp", ("context", "tensor"), None),
            P(("context", "tensor"), None),
            P("tensor", None, None),
            P("tensor", None, None),
            P("tensor", None, None),
            P("tensor", None, None),
        ),
        check_vma=False,
    )
```

```python
import math

import jax
import jax.numpy as jnp
from jax import lax
from jax.sharding import PartitionSpec as P

table_mode = lax.Precision.DEFAULT


def blockwise(acts, weight):
    rows = acts.shape[0]
    shaped = acts.reshape(rows, weight.shape[0], weight.shape[1])
    return jnp.einsum("tni,nij->tnj", shaped, weight, preferred_element_type=jnp.float32).reshape(
        rows, -1
    )


def blockwise_back(acts, weight):
    rows = acts.shape[0]
    shaped = acts.reshape(rows, weight.shape[0], weight.shape[1])
    return jnp.einsum("tnj,nij->tni", shaped, weight, preferred_element_type=jnp.float32).reshape(
        rows, -1
    )


def weight_term(inputs, grads, blocks):
    rows = inputs.shape[0]
    left = inputs.reshape(rows, blocks, -1)
    right = grads.reshape(rows, blocks, -1)
    return jnp.einsum("tni,tnj->nij", left, right, preferred_element_type=jnp.float32)


def angle_table(rows, cols, total):
    product = (
        jnp.arange(rows, dtype=jnp.int32)[:, None]
        * jnp.arange(cols, dtype=jnp.int32)[None, :]
        % total
    )
    angle = product.astype(jnp.float32) * (2.0 * math.pi / total)
    return (jnp.cos(angle), jnp.sin(angle))


def make_tables(length):
    second = length // 128
    cosine_first, sine_first = angle_table(128, 128, 128)
    cosine_second, sine_second = angle_table(second, second, second)
    cosine_twist, sine_twist = angle_table(128, second, length)
    return (
        cosine_first,
        sine_first,
        cosine_second,
        sine_second,
        cosine_twist[:, :, None],
        sine_twist[:, :, None],
    )


def across_first(matrix, array):
    return jnp.einsum(
        "kn,nmc->kmc", matrix, array, precision=table_mode, preferred_element_type=jnp.float32
    )


def across_second(array, matrix):
    return jnp.einsum(
        "kmc,ml->klc", array, matrix, precision=table_mode, preferred_element_type=jnp.float32
    )


def forward_transform(signal, tables):
    cosine_first, sine_first, cosine_second, sine_second, cosine_twist, sine_twist = tables
    half = cosine_first.shape[0] // 2
    shaped = signal.reshape(half, cosine_second.shape[0], signal.shape[1])
    real_section = across_first(cosine_first[:, :half], shaped)
    imag_section = -across_first(sine_first[:, :half], shaped)
    real_turned = real_section * cosine_twist + imag_section * sine_twist
    imag_turned = imag_section * cosine_twist - real_section * sine_twist
    real_out = across_second(real_turned, cosine_second) + across_second(imag_turned, sine_second)
    imag_out = across_second(imag_turned, cosine_second) - across_second(real_turned, sine_second)
    return (real_out, imag_out)


def inverse_transform(real_spec, imag_spec, tables):
    cosine_first, sine_first, cosine_second, sine_second, cosine_twist, sine_twist = tables
    half = cosine_first.shape[0] // 2
    total = cosine_first.shape[0] * cosine_second.shape[0]
    real_section = across_second(real_spec, cosine_second) - across_second(imag_spec, sine_second)
    imag_section = across_second(imag_spec, cosine_second) + across_second(real_spec, sine_second)
    real_turned = real_section * cosine_twist - imag_section * sine_twist
    imag_turned = imag_section * cosine_twist + real_section * sine_twist
    signal = (
        across_first(cosine_first[:half], real_turned)
        - across_first(sine_first[:half], imag_turned)
    ) / total
    return signal.reshape(half * cosine_second.shape[0], -1)


def spectral_tables(length):
    first = 128
    second = length // first
    half = first // 2
    cosine_first, sine_first = angle_table(first, first, first)
    cosine_second, sine_second = angle_table(second, second, second)
    cosine_twist, sine_twist = angle_table(first, second, length)
    forward_first = jnp.concatenate([cosine_first[:, :half], -sine_first[:, :half]], axis=0)
    forward_second = jnp.stack(
        [
            jnp.stack([cosine_second, -sine_second], axis=1),
            jnp.stack([sine_second, cosine_second], axis=1),
        ]
    )
    inverse_second = jnp.stack(
        [
            jnp.stack([cosine_second, sine_second], axis=1),
            jnp.stack([-sine_second, cosine_second], axis=1),
        ]
    )
    inverse_first = jnp.stack([cosine_first[:half], -sine_first[:half]], axis=1) / length
    return (
        forward_first,
        forward_second,
        inverse_second,
        inverse_first,
        cosine_twist[:, :, None],
        sine_twist[:, :, None],
    )


def spectra(signal, tables):
    forward_first, forward_second, _, _, cosine_twist, sine_twist = tables
    first = cosine_twist.shape[0]
    half = first // 2
    shaped = signal.reshape(half, cosine_twist.shape[1], signal.shape[1])
    section = jnp.einsum(
        "kn,nmc->kmc", forward_first, shaped, precision=table_mode,
        preferred_element_type=jnp.float32,
    )
    real_section, imag_section = section[:first], section[first:]
    turned = jnp.stack(
        [
            real_section * cosine_twist + imag_section * sine_twist,
            imag_section * cosine_twist - real_section * sine_twist,
        ]
    )
    return jnp.einsum(
        "rkmc,rmsl->sklc", turned, forward_second, precision=table_mode,
        preferred_element_type=jnp.float32,
    )


def signals(spec, tables):
    _, _, inverse_second, inverse_first, cosine_twist, sine_twist = tables
    section = jnp.einsum(
        "sklc,slrm->rkmc", spec, inverse_second, precision=table_mode,
        preferred_element_type=jnp.float32,
    )
    real_section, imag_section = section[0], section[1]
    turned = jnp.stack(
        [
            real_section * cosine_twist - imag_section * sine_twist,
            imag_section * cosine_twist + real_section * sine_twist,
        ]
    )
    out = jnp.einsum(
        "nrk,rkmc->nmc", inverse_first, turned, precision=table_mode,
        preferred_element_type=jnp.float32,
    )
    return out.reshape(-1, out.shape[-1])


def shards(
    tokens, filter_taps, query_weight, key_weight, value_weight, output_weight, out_cotangent
):
    ctx = lax.axis_size("context")
    ten = lax.axis_size("tensor")
    rows = tokens.shape[1]
    arrived = lax.all_to_all(
        jnp.concatenate(
            [tokens[0], out_cotangent[0], filter_taps.astype(jnp.bfloat16)], axis=0
        ),
        "tensor",
        split_axis=1,
        concat_axis=0,
        tiled=True,
    )
    arrived = arrived.reshape(ten, 3, rows, arrived.shape[1])
    inputs = arrived[:, 0].reshape(ten * rows, -1)
    upstream = arrived[:, 1].reshape(ten * rows, -1)
    taps_mid = arrived[:, 2].reshape(ten * rows, -1)
    blocks = query_weight.shape[0]
    query = blockwise(inputs, query_weight).astype(jnp.bfloat16)
    keys = blockwise(inputs, key_weight).astype(jnp.bfloat16)
    values = blockwise(inputs, value_weight).astype(jnp.bfloat16)
    gated = (keys.astype(jnp.float32) * values.astype(jnp.float32)).astype(jnp.bfloat16)
    query_wide = query.astype(jnp.float32)
    back_weighted = blockwise_back(upstream, output_weight)
    conv_grad = (back_weighted * query_wide).astype(jnp.bfloat16)
    local = inputs.shape[0]
    timed = lax.all_to_all(
        jnp.concatenate([gated, conv_grad, taps_mid], axis=0),
        "context",
        split_axis=1,
        concat_axis=0,
        tiled=True,
    )
    timed = timed.reshape(ctx, 3, local, timed.shape[1])
    gated_time = timed[:, 0].reshape(ctx * local, -1)
    grad_time = timed[:, 1].reshape(ctx * local, -1)
    taps = timed[:, 2].reshape(ctx * local, -1).astype(jnp.float32)
    length = taps.shape[0]
    width = taps.shape[1]
    tables = spectral_tables(2 * length)
    spec = spectra(
        jnp.concatenate(
            [taps, gated_time.astype(jnp.float32), grad_time.astype(jnp.float32)], axis=1
        ),
        tables,
    )
    real_spec, imag_spec = spec[0], spec[1]
    real_taps, real_gated, real_grad = (
        real_spec[..., :width], real_spec[..., width : 2 * width], real_spec[..., 2 * width :]
    )
    imag_taps, imag_gated, imag_grad = (
        imag_spec[..., :width], imag_spec[..., width : 2 * width], imag_spec[..., 2 * width :]
    )
    products = jnp.stack(
        [
            jnp.concatenate(
                [
                    real_taps * real_gated - imag_taps * imag_gated,
                    real_taps * real_grad + imag_taps * imag_grad,
                    real_grad * real_gated + imag_grad * imag_gated,
                ],
                axis=-1,
            ),
            jnp.concatenate(
                [
                    real_taps * imag_gated + imag_taps * real_gated,
                    real_taps * imag_grad - imag_taps * real_grad,
                    imag_grad * real_gated - real_grad * imag_gated,
                ],
                axis=-1,
            ),
        ]
    )
    results = signals(products, tables)
    conv_time = results[:, :width]
    gated_time_back = results[:, width : 2 * width]
    taps_back = results[:, 2 * width :]
    returned = lax.all_to_all(
        jnp.stack(
            [
                conv_time.astype(jnp.bfloat16).reshape(ctx, local, width),
                gated_time_back.astype(jnp.bfloat16).reshape(ctx, local, width),
            ],
            axis=1,
        ).reshape(ctx * 2 * local, width),
        "context",
        split_axis=0,
        concat_axis=1,
        tiled=True,
    )
    conv, gated_narrow = returned[:local], returned[local:]
    conv_wide = conv.astype(jnp.float32)
    weighted = (query_wide * conv_wide).astype(jnp.bfloat16)
    query_back = (back_weighted * conv_wide).astype(jnp.bfloat16)
    gated_back = gated_narrow.astype(jnp.float32)
    key_back = (gated_back * values.astype(jnp.float32)).astype(jnp.bfloat16)
    value_back = (gated_back * keys.astype(jnp.float32)).astype(jnp.bfloat16)
    factor = 1.0 / math.sqrt(lax.axis_size("dp") * length)
    terms = (
        (weight_term(inputs, query_back, blocks) * factor).astype(jnp.bfloat16),
        (weight_term(inputs, key_back, blocks) * factor).astype(jnp.bfloat16),
        (weight_term(inputs, value_back, blocks) * factor).astype(jnp.bfloat16),
        (weight_term(weighted, upstream, blocks) * factor).astype(jnp.bfloat16),
    )
    terms, (query_back, key_back, value_back, weighted) = lax.optimization_barrier(
        (terms, (query_back, key_back, value_back, weighted))
    )
    group = ("dp", "context")
    members = lax.axis_size("dp") * lax.axis_size("context")
    pieces = lax.all_to_all(
        jnp.concatenate([term.reshape(members, -1) for term in terms], axis=1),
        group,
        split_axis=0,
        concat_axis=0,
        tiled=True,
    )
    own = jnp.sum(pieces.astype(jnp.float32), axis=0).astype(jnp.bfloat16)
    gathered = lax.all_to_all(
        jnp.broadcast_to(own[None], (members, own.shape[0])),
        group,
        split_axis=0,
        concat_axis=0,
        tiled=True,
    ).astype(jnp.float32)
    share = gathered.shape[1] // len(terms)
    query_grad, key_grad, value_grad, output_grad = (
        gathered[:, index * share : (index + 1) * share].reshape(terms[index].shape)
        for index in range(len(terms))
    )
    mixed = blockwise(weighted, output_weight).astype(jnp.bfloat16)
    token_grad = (
        blockwise_back(query_back, query_weight)
        + blockwise_back(key_back, key_weight)
        + blockwise_back(value_back, value_weight)
    ).astype(jnp.bfloat16)
    taps_total = lax.psum((taps_back * factor).astype(jnp.bfloat16), "dp")
    filter_mid = lax.all_to_all(taps_total, "context", split_axis=0, concat_axis=1, tiled=True)
    leaving = lax.all_to_all(
        jnp.stack(
            [
                part.reshape(ten, rows, part.shape[1])
                for part in (mixed, token_grad, filter_mid)
            ],
            axis=1,
        ).reshape(ten * 3 * rows, -1),
        "tensor",
        split_axis=0,
        concat_axis=1,
        tiled=True,
    )
    mixed_rows = leaving[:rows]
    grad_rows = leaving[rows : 2 * rows]
    filter_grad = leaving[2 * rows :].astype(jnp.float32)
    return (
        mixed_rows[None],
        grad_rows[None],
        filter_grad,
        query_grad,
        key_grad,
        value_grad,
        output_grad,
    )


def solution(mesh):
    placed = (
        P("dp", ("context", "tensor"), None),
        P(("context", "tensor"), None),
        P("tensor", None, None),
        P("tensor", None, None),
        P("tensor", None, None),
        P("tensor", None, None),
        P("dp", ("context", "tensor"), None),
    )
    return jax.shard_map(
        shards,
        mesh=mesh,
        in_specs=placed,
        out_specs=(
            P("dp", ("context", "tensor"), None),
            P("dp", ("context", "tensor"), None),
            P(("context", "tensor"), None),
            P("tensor", None, None),
            P("tensor", None, None),
            P("tensor", None, None),
            P("tensor", None, None),
        ),
        check_vma=False,
    )
```

```python
import math

import jax
import jax.numpy as jnp
from jax import lax
from jax.sharding import PartitionSpec as P

table_mode = lax.Precision.DEFAULT


def blockwise(acts, weight):
    rows = acts.shape[0]
    shaped = acts.reshape(rows, weight.shape[0], weight.shape[1])
    return jnp.einsum("tni,nij->tnj", shaped, weight, preferred_element_type=jnp.float32).reshape(
        rows, -1
    )


def blockwise_back(acts, weight):
    rows = acts.shape[0]
    shaped = acts.reshape(rows, weight.shape[0], weight.shape[1])
    return jnp.einsum("tnj,nij->tni", shaped, weight, preferred_element_type=jnp.float32).reshape(
        rows, -1
    )


def weight_term(inputs, grads, blocks):
    rows = inputs.shape[0]
    left = inputs.reshape(rows, blocks, -1)
    right = grads.reshape(rows, blocks, -1)
    return jnp.einsum("tni,tnj->nij", left, right, preferred_element_type=jnp.float32)


def angle_table(rows, cols, total):
    product = (
        jnp.arange(rows, dtype=jnp.int32)[:, None]
        * jnp.arange(cols, dtype=jnp.int32)[None, :]
        % total
    )
    angle = product.astype(jnp.float32) * (2.0 * math.pi / total)
    return (jnp.cos(angle), jnp.sin(angle))


def make_tables(length):
    second = length // 128
    cosine_first, sine_first = angle_table(128, 128, 128)
    cosine_second, sine_second = angle_table(second, second, second)
    cosine_twist, sine_twist = angle_table(128, second, length)
    return (
        cosine_first,
        sine_first,
        cosine_second,
        sine_second,
        cosine_twist[:, :, None],
        sine_twist[:, :, None],
    )


def across_first(matrix, array):
    return jnp.einsum(
        "kn,nmc->kmc", matrix, array, precision=table_mode, preferred_element_type=jnp.float32
    )


def across_second(array, matrix):
    return jnp.einsum(
        "kmc,ml->klc", array, matrix, precision=table_mode, preferred_element_type=jnp.float32
    )


def forward_transform(signal, tables):
    cosine_first, sine_first, cosine_second, sine_second, cosine_twist, sine_twist = tables
    half = cosine_first.shape[0] // 2
    shaped = signal.reshape(half, cosine_second.shape[0], signal.shape[1])
    real_section = across_first(cosine_first[:, :half], shaped)
    imag_section = -across_first(sine_first[:, :half], shaped)
    real_turned = real_section * cosine_twist + imag_section * sine_twist
    imag_turned = imag_section * cosine_twist - real_section * sine_twist
    real_out = across_second(real_turned, cosine_second) + across_second(imag_turned, sine_second)
    imag_out = across_second(imag_turned, cosine_second) - across_second(real_turned, sine_second)
    return (real_out, imag_out)


def inverse_transform(real_spec, imag_spec, tables):
    cosine_first, sine_first, cosine_second, sine_second, cosine_twist, sine_twist = tables
    half = cosine_first.shape[0] // 2
    total = cosine_first.shape[0] * cosine_second.shape[0]
    real_section = across_second(real_spec, cosine_second) - across_second(imag_spec, sine_second)
    imag_section = across_second(imag_spec, cosine_second) + across_second(real_spec, sine_second)
    real_turned = real_section * cosine_twist - imag_section * sine_twist
    imag_turned = imag_section * cosine_twist + real_section * sine_twist
    signal = (
        across_first(cosine_first[:half], real_turned)
        - across_first(sine_first[:half], imag_turned)
    ) / total
    return signal.reshape(half * cosine_second.shape[0], -1)


def spectral_tables(length):
    first = 128
    second = length // first
    half = first // 2
    cosine_first, sine_first = angle_table(first, first, first)
    cosine_second, sine_second = angle_table(second, second, second)
    cosine_twist, sine_twist = angle_table(first, second, length)
    forward_first = jnp.concatenate([cosine_first[:, :half], -sine_first[:, :half]], axis=0)
    forward_second = jnp.stack(
        [
            jnp.stack([cosine_second, -sine_second], axis=1),
            jnp.stack([sine_second, cosine_second], axis=1),
        ]
    )
    inverse_second = jnp.stack(
        [
            jnp.stack([cosine_second, sine_second], axis=1),
            jnp.stack([-sine_second, cosine_second], axis=1),
        ]
    )
    inverse_first = jnp.stack([cosine_first[:half], -sine_first[:half]], axis=1) / length
    return (
        forward_first,
        forward_second,
        inverse_second,
        inverse_first,
        cosine_twist[:, :, None],
        sine_twist[:, :, None],
    )


def spectra(signal, tables):
    forward_first, forward_second, _, _, cosine_twist, sine_twist = tables
    first = cosine_twist.shape[0]
    half = first // 2
    shaped = signal.reshape(half, cosine_twist.shape[1], signal.shape[1])
    section = jnp.einsum(
        "kn,nmc->kmc", forward_first, shaped, precision=table_mode,
        preferred_element_type=jnp.float32,
    )
    real_section, imag_section = section[:first], section[first:]
    turned = jnp.stack(
        [
            real_section * cosine_twist + imag_section * sine_twist,
            imag_section * cosine_twist - real_section * sine_twist,
        ]
    )
    return jnp.einsum(
        "rkmc,rmsl->sklc", turned, forward_second, precision=table_mode,
        preferred_element_type=jnp.float32,
    )


def signals(spec, tables):
    _, _, inverse_second, inverse_first, cosine_twist, sine_twist = tables
    section = jnp.einsum(
        "sklc,slrm->rkmc", spec, inverse_second, precision=table_mode,
        preferred_element_type=jnp.float32,
    )
    real_section, imag_section = section[0], section[1]
    turned = jnp.stack(
        [
            real_section * cosine_twist - imag_section * sine_twist,
            imag_section * cosine_twist + real_section * sine_twist,
        ]
    )
    out = jnp.einsum(
        "nrk,rkmc->nmc", inverse_first, turned, precision=table_mode,
        preferred_element_type=jnp.float32,
    )
    return out.reshape(-1, out.shape[-1])


def shards(
    tokens, filter_taps, query_weight, key_weight, value_weight, output_weight, out_cotangent
):
    ctx = lax.axis_size("context")
    ten = lax.axis_size("tensor")
    rows = tokens.shape[1]
    arrived = lax.all_to_all(
        jnp.concatenate(
            [tokens[0], out_cotangent[0], filter_taps.astype(jnp.bfloat16)], axis=0
        ),
        "tensor",
        split_axis=1,
        concat_axis=0,
        tiled=True,
    )
    arrived = arrived.reshape(ten, 3, rows, arrived.shape[1])
    inputs = arrived[:, 0].reshape(ten * rows, -1)
    upstream = arrived[:, 1].reshape(ten * rows, -1)
    taps_mid = arrived[:, 2].reshape(ten * rows, -1)
    blocks = query_weight.shape[0]
    query = blockwise(inputs, query_weight).astype(jnp.bfloat16)
    keys = blockwise(inputs, key_weight).astype(jnp.bfloat16)
    values = blockwise(inputs, value_weight).astype(jnp.bfloat16)
    gated = (keys.astype(jnp.float32) * values.astype(jnp.float32)).astype(jnp.bfloat16)
    query_wide = query.astype(jnp.float32)
    back_weighted = blockwise_back(upstream, output_weight)
    conv_grad = (back_weighted * query_wide).astype(jnp.bfloat16)
    local = inputs.shape[0]
    timed = lax.all_to_all(
        jnp.concatenate([gated, conv_grad, taps_mid], axis=0),
        "context",
        split_axis=1,
        concat_axis=0,
        tiled=True,
    )
    timed = timed.reshape(ctx, 3, local, timed.shape[1])
    gated_time = timed[:, 0].reshape(ctx * local, -1)
    grad_time = timed[:, 1].reshape(ctx * local, -1)
    taps = timed[:, 2].reshape(ctx * local, -1).astype(jnp.float32)
    length = taps.shape[0]
    width = taps.shape[1]
    tables = spectral_tables(2 * length)
    spec = spectra(
        jnp.concatenate(
            [taps, gated_time.astype(jnp.float32), grad_time.astype(jnp.float32)], axis=1
        ),
        tables,
    )
    real_spec, imag_spec = spec[0], spec[1]
    real_taps, real_gated, real_grad = (
        real_spec[..., :width], real_spec[..., width : 2 * width], real_spec[..., 2 * width :]
    )
    imag_taps, imag_gated, imag_grad = (
        imag_spec[..., :width], imag_spec[..., width : 2 * width], imag_spec[..., 2 * width :]
    )
    products = jnp.stack(
        [
            jnp.concatenate(
                [
                    real_taps * real_gated - imag_taps * imag_gated,
                    real_taps * real_grad + imag_taps * imag_grad,
                    real_grad * real_gated + imag_grad * imag_gated,
                ],
                axis=-1,
            ),
            jnp.concatenate(
                [
                    real_taps * imag_gated + imag_taps * real_gated,
                    real_taps * imag_grad - imag_taps * real_grad,
                    imag_grad * real_gated - real_grad * imag_gated,
                ],
                axis=-1,
            ),
        ]
    )
    results = signals(products, tables)
    conv_time = results[:, :width]
    gated_time_back = results[:, width : 2 * width]
    taps_back = results[:, 2 * width :]
    returned = lax.all_to_all(
        jnp.stack(
            [
                conv_time.astype(jnp.bfloat16).reshape(ctx, local, width),
                gated_time_back.astype(jnp.bfloat16).reshape(ctx, local, width),
            ],
            axis=1,
        ).reshape(ctx * 2 * local, width),
        "context",
        split_axis=0,
        concat_axis=1,
        tiled=True,
    )
    conv, gated_narrow = returned[:local], returned[local:]
    conv_wide = conv.astype(jnp.float32)
    weighted = (query_wide * conv_wide).astype(jnp.bfloat16)
    query_back = (back_weighted * conv_wide).astype(jnp.bfloat16)
    gated_back = gated_narrow.astype(jnp.float32)
    key_back = (gated_back * values.astype(jnp.float32)).astype(jnp.bfloat16)
    value_back = (gated_back * keys.astype(jnp.float32)).astype(jnp.bfloat16)
    factor = 1.0 / math.sqrt(lax.axis_size("dp") * length)
    terms = (
        (weight_term(inputs, query_back, blocks) * factor).astype(jnp.bfloat16),
        (weight_term(inputs, key_back, blocks) * factor).astype(jnp.bfloat16),
        (weight_term(inputs, value_back, blocks) * factor).astype(jnp.bfloat16),
        (weight_term(weighted, upstream, blocks) * factor).astype(jnp.bfloat16),
    )
    terms, (query_back, key_back, value_back, weighted) = lax.optimization_barrier(
        (terms, (query_back, key_back, value_back, weighted))
    )
    pair = lax.axis_index("dp")
    swap = [(0, 1), (1, 0)]
    flat = jnp.concatenate([term.reshape(2, -1) for term in terms], axis=1)
    kept = lax.dynamic_index_in_dim(flat, pair, axis=0, keepdims=False)
    given = lax.dynamic_index_in_dim(flat, 1 - pair, axis=0, keepdims=False)
    taken = lax.ppermute(given, "dp", swap)
    half = (kept.astype(jnp.float32) + taken.astype(jnp.float32)).astype(jnp.bfloat16)
    half = lax.psum(half, "context")
    other = lax.ppermute(half, "dp", swap)
    whole = jnp.where(pair == 0, jnp.stack([half, other]), jnp.stack([other, half]))
    share = whole.shape[1] // len(terms)
    query_grad, key_grad, value_grad, output_grad = (
        whole[:, index * share : (index + 1) * share]
        .reshape(terms[index].shape)
        .astype(jnp.float32)
        for index in range(len(terms))
    )
    mixed = blockwise(weighted, output_weight).astype(jnp.bfloat16)
    token_grad = (
        blockwise_back(query_back, query_weight)
        + blockwise_back(key_back, key_weight)
        + blockwise_back(value_back, value_weight)
    ).astype(jnp.bfloat16)
    taps_part = (taps_back * factor).astype(jnp.bfloat16)
    taps_total = (
        taps_part.astype(jnp.float32) + lax.ppermute(taps_part, "dp", swap).astype(jnp.float32)
    ).astype(jnp.bfloat16)
    filter_mid = lax.all_to_all(taps_total, "context", split_axis=0, concat_axis=1, tiled=True)
    leaving = lax.all_to_all(
        jnp.stack(
            [
                part.reshape(ten, rows, part.shape[1])
                for part in (mixed, token_grad, filter_mid)
            ],
            axis=1,
        ).reshape(ten * 3 * rows, -1),
        "tensor",
        split_axis=0,
        concat_axis=1,
        tiled=True,
    )
    mixed_rows = leaving[:rows]
    grad_rows = leaving[rows : 2 * rows]
    filter_grad = leaving[2 * rows :].astype(jnp.float32)
    return (
        mixed_rows[None],
        grad_rows[None],
        filter_grad,
        query_grad,
        key_grad,
        value_grad,
        output_grad,
    )


def solution(mesh):
    placed = (
        P("dp", ("context", "tensor"), None),
        P(("context", "tensor"), None),
        P("tensor", None, None),
        P("tensor", None, None),
        P("tensor", None, None),
        P("tensor", None, None),
        P("dp", ("context", "tensor"), None),
    )
    return jax.shard_map(
        shards,
        mesh=mesh,
        in_specs=placed,
        out_specs=(
            P("dp", ("context", "tensor"), None),
            P("dp", ("context", "tensor"), None),
            P(("context", "tensor"), None),
            P("tensor", None, None),
            P("tensor", None, None),
            P("tensor", None, None),
            P("tensor", None, None),
        ),
        check_vma=False,
    )
```

```python
import math

import jax
import jax.numpy as jnp
from jax import lax
from jax.sharding import PartitionSpec as P

table_mode = lax.Precision.DEFAULT


def blockwise(acts, weight):
    rows = acts.shape[0]
    shaped = acts.reshape(rows, weight.shape[0], weight.shape[1])
    return jnp.einsum("tni,nij->tnj", shaped, weight, preferred_element_type=jnp.float32).reshape(
        rows, -1
    )


def blockwise_back(acts, weight):
    rows = acts.shape[0]
    shaped = acts.reshape(rows, weight.shape[0], weight.shape[1])
    return jnp.einsum("tnj,nij->tni", shaped, weight, preferred_element_type=jnp.float32).reshape(
        rows, -1
    )


def weight_term(inputs, grads, blocks):
    rows = inputs.shape[0]
    left = inputs.reshape(rows, blocks, -1)
    right = grads.reshape(rows, blocks, -1)
    return jnp.einsum("tni,tnj->nij", left, right, preferred_element_type=jnp.float32)


def angle_table(rows, cols, total):
    product = (
        jnp.arange(rows, dtype=jnp.int32)[:, None]
        * jnp.arange(cols, dtype=jnp.int32)[None, :]
        % total
    )
    angle = product.astype(jnp.float32) * (2.0 * math.pi / total)
    return (jnp.cos(angle), jnp.sin(angle))


def make_tables(length):
    second = length // 128
    cosine_first, sine_first = angle_table(128, 128, 128)
    cosine_second, sine_second = angle_table(second, second, second)
    cosine_twist, sine_twist = angle_table(128, second, length)
    return (
        cosine_first,
        sine_first,
        cosine_second,
        sine_second,
        cosine_twist[:, :, None],
        sine_twist[:, :, None],
    )


def across_first(matrix, array):
    return jnp.einsum(
        "kn,nmc->kmc", matrix, array, precision=table_mode, preferred_element_type=jnp.float32
    )


def across_second(array, matrix):
    return jnp.einsum(
        "kmc,ml->klc", array, matrix, precision=table_mode, preferred_element_type=jnp.float32
    )


def forward_transform(signal, tables):
    cosine_first, sine_first, cosine_second, sine_second, cosine_twist, sine_twist = tables
    half = cosine_first.shape[0] // 2
    shaped = signal.reshape(half, cosine_second.shape[0], signal.shape[1])
    real_section = across_first(cosine_first[:, :half], shaped)
    imag_section = -across_first(sine_first[:, :half], shaped)
    real_turned = real_section * cosine_twist + imag_section * sine_twist
    imag_turned = imag_section * cosine_twist - real_section * sine_twist
    real_out = across_second(real_turned, cosine_second) + across_second(imag_turned, sine_second)
    imag_out = across_second(imag_turned, cosine_second) - across_second(real_turned, sine_second)
    return (real_out, imag_out)


def inverse_transform(real_spec, imag_spec, tables):
    cosine_first, sine_first, cosine_second, sine_second, cosine_twist, sine_twist = tables
    half = cosine_first.shape[0] // 2
    total = cosine_first.shape[0] * cosine_second.shape[0]
    real_section = across_second(real_spec, cosine_second) - across_second(imag_spec, sine_second)
    imag_section = across_second(imag_spec, cosine_second) + across_second(real_spec, sine_second)
    real_turned = real_section * cosine_twist - imag_section * sine_twist
    imag_turned = imag_section * cosine_twist + real_section * sine_twist
    signal = (
        across_first(cosine_first[:half], real_turned)
        - across_first(sine_first[:half], imag_turned)
    ) / total
    return signal.reshape(half * cosine_second.shape[0], -1)


def spectral_tables(length):
    first = 128
    second = length // first
    half = first // 2
    cosine_first, sine_first = angle_table(first, first, first)
    cosine_second, sine_second = angle_table(second, second, second)
    cosine_twist, sine_twist = angle_table(first, second, length)
    forward_first = jnp.concatenate([cosine_first[:, :half], -sine_first[:, :half]], axis=0)
    forward_second = jnp.stack(
        [
            jnp.stack([cosine_second, -sine_second], axis=1),
            jnp.stack([sine_second, cosine_second], axis=1),
        ]
    )
    inverse_second = jnp.stack(
        [
            jnp.stack([cosine_second, sine_second], axis=1),
            jnp.stack([-sine_second, cosine_second], axis=1),
        ]
    )
    inverse_first = jnp.stack([cosine_first[:half], -sine_first[:half]], axis=1) / length
    return (
        forward_first,
        forward_second,
        inverse_second,
        inverse_first,
        cosine_twist[:, :, None],
        sine_twist[:, :, None],
    )


def spectra(signal, tables):
    forward_first, forward_second, _, _, cosine_twist, sine_twist = tables
    first = cosine_twist.shape[0]
    half = first // 2
    shaped = signal.reshape(half, cosine_twist.shape[1], signal.shape[1])
    section = jnp.einsum(
        "kn,nmc->kmc", forward_first.astype(jnp.bfloat16), shaped.astype(jnp.bfloat16),
        precision=table_mode,
        preferred_element_type=jnp.float32,
    )
    real_section, imag_section = section[:first], section[first:]
    turned = jnp.stack(
        [
            real_section * cosine_twist + imag_section * sine_twist,
            imag_section * cosine_twist - real_section * sine_twist,
        ]
    ).astype(jnp.bfloat16)
    return jnp.einsum(
        "rkmc,rmsl->sklc", turned, forward_second.astype(jnp.bfloat16), precision=table_mode,
        preferred_element_type=jnp.float32,
    )


def signals(spec, tables):
    _, _, inverse_second, inverse_first, cosine_twist, sine_twist = tables
    section = jnp.einsum(
        "sklc,slrm->rkmc", spec, inverse_second.astype(jnp.bfloat16), precision=table_mode,
        preferred_element_type=jnp.float32,
    )
    real_section, imag_section = section[0], section[1]
    turned = jnp.stack(
        [
            real_section * cosine_twist - imag_section * sine_twist,
            imag_section * cosine_twist + real_section * sine_twist,
        ]
    ).astype(jnp.bfloat16)
    out = jnp.einsum(
        "nrk,rkmc->nmc", inverse_first.astype(jnp.bfloat16), turned, precision=table_mode,
        preferred_element_type=jnp.float32,
    )
    return out.reshape(-1, out.shape[-1])


def shards(
    tokens, filter_taps, query_weight, key_weight, value_weight, output_weight, out_cotangent
):
    ctx = lax.axis_size("context")
    ten = lax.axis_size("tensor")
    rows = tokens.shape[1]
    arrived = lax.all_to_all(
        jnp.concatenate(
            [tokens[0], out_cotangent[0], filter_taps.astype(jnp.bfloat16)], axis=0
        ),
        "tensor",
        split_axis=1,
        concat_axis=0,
        tiled=True,
    )
    arrived = arrived.reshape(ten, 3, rows, arrived.shape[1])
    inputs = arrived[:, 0].reshape(ten * rows, -1)
    upstream = arrived[:, 1].reshape(ten * rows, -1)
    taps_mid = arrived[:, 2].reshape(ten * rows, -1)
    blocks = query_weight.shape[0]
    query = blockwise(inputs, query_weight).astype(jnp.bfloat16)
    keys = blockwise(inputs, key_weight).astype(jnp.bfloat16)
    values = blockwise(inputs, value_weight).astype(jnp.bfloat16)
    gated = (keys.astype(jnp.float32) * values.astype(jnp.float32)).astype(jnp.bfloat16)
    query_wide = query.astype(jnp.float32)
    back_weighted = blockwise_back(upstream, output_weight)
    conv_grad = (back_weighted * query_wide).astype(jnp.bfloat16)
    local = inputs.shape[0]
    timed = lax.all_to_all(
        jnp.concatenate([gated, conv_grad, taps_mid], axis=0),
        "context",
        split_axis=1,
        concat_axis=0,
        tiled=True,
    )
    timed = timed.reshape(ctx, 3, local, timed.shape[1])
    gated_time = timed[:, 0].reshape(ctx * local, -1)
    grad_time = timed[:, 1].reshape(ctx * local, -1)
    taps = timed[:, 2].reshape(ctx * local, -1).astype(jnp.float32)
    length = taps.shape[0]
    width = taps.shape[1]
    tables = spectral_tables(2 * length)
    spec = spectra(
        jnp.concatenate(
            [taps, gated_time.astype(jnp.float32), grad_time.astype(jnp.float32)], axis=1
        ),
        tables,
    )
    real_spec, imag_spec = spec[0], spec[1]
    real_taps, real_gated, real_grad = (
        real_spec[..., :width], real_spec[..., width : 2 * width], real_spec[..., 2 * width :]
    )
    imag_taps, imag_gated, imag_grad = (
        imag_spec[..., :width], imag_spec[..., width : 2 * width], imag_spec[..., 2 * width :]
    )
    products = jnp.stack(
        [
            jnp.concatenate(
                [
                    real_taps * real_gated - imag_taps * imag_gated,
                    real_taps * real_grad + imag_taps * imag_grad,
                    real_grad * real_gated + imag_grad * imag_gated,
                ],
                axis=-1,
            ),
            jnp.concatenate(
                [
                    real_taps * imag_gated + imag_taps * real_gated,
                    real_taps * imag_grad - imag_taps * real_grad,
                    imag_grad * real_gated - real_grad * imag_gated,
                ],
                axis=-1,
            ),
        ]
    ).astype(jnp.bfloat16)
    results = signals(products, tables)
    conv_time = results[:, :width]
    gated_time_back = results[:, width : 2 * width]
    taps_back = results[:, 2 * width :]
    returned = lax.all_to_all(
        jnp.stack(
            [
                conv_time.astype(jnp.bfloat16).reshape(ctx, local, width),
                gated_time_back.astype(jnp.bfloat16).reshape(ctx, local, width),
            ],
            axis=1,
        ).reshape(ctx * 2 * local, width),
        "context",
        split_axis=0,
        concat_axis=1,
        tiled=True,
    )
    conv, gated_narrow = returned[:local], returned[local:]
    conv_wide = conv.astype(jnp.float32)
    weighted = (query_wide * conv_wide).astype(jnp.bfloat16)
    query_back = (back_weighted * conv_wide).astype(jnp.bfloat16)
    gated_back = gated_narrow.astype(jnp.float32)
    key_back = (gated_back * values.astype(jnp.float32)).astype(jnp.bfloat16)
    value_back = (gated_back * keys.astype(jnp.float32)).astype(jnp.bfloat16)
    factor = 1.0 / math.sqrt(lax.axis_size("dp") * length)
    terms = (
        (weight_term(inputs, query_back, blocks) * factor).astype(jnp.bfloat16),
        (weight_term(inputs, key_back, blocks) * factor).astype(jnp.bfloat16),
        (weight_term(inputs, value_back, blocks) * factor).astype(jnp.bfloat16),
        (weight_term(weighted, upstream, blocks) * factor).astype(jnp.bfloat16),
    )
    terms, (query_back, key_back, value_back, weighted) = lax.optimization_barrier(
        (terms, (query_back, key_back, value_back, weighted))
    )
    query_grad, key_grad, value_grad, output_grad = (
        lax.psum(term, ("dp", "context")).astype(jnp.float32) for term in terms
    )
    mixed = blockwise(weighted, output_weight).astype(jnp.bfloat16)
    token_grad = (
        blockwise_back(query_back, query_weight)
        + blockwise_back(key_back, key_weight)
        + blockwise_back(value_back, value_weight)
    ).astype(jnp.bfloat16)
    taps_total = lax.psum((taps_back * factor).astype(jnp.bfloat16), "dp")
    filter_mid = lax.all_to_all(taps_total, "context", split_axis=0, concat_axis=1, tiled=True)
    leaving = lax.all_to_all(
        jnp.stack(
            [
                part.reshape(ten, rows, part.shape[1])
                for part in (mixed, token_grad, filter_mid)
            ],
            axis=1,
        ).reshape(ten * 3 * rows, -1),
        "tensor",
        split_axis=0,
        concat_axis=1,
        tiled=True,
    )
    mixed_rows = leaving[:rows]
    grad_rows = leaving[rows : 2 * rows]
    filter_grad = leaving[2 * rows :].astype(jnp.float32)
    return (
        mixed_rows[None],
        grad_rows[None],
        filter_grad,
        query_grad,
        key_grad,
        value_grad,
        output_grad,
    )


def solution(mesh):
    placed = (
        P("dp", ("context", "tensor"), None),
        P(("context", "tensor"), None),
        P("tensor", None, None),
        P("tensor", None, None),
        P("tensor", None, None),
        P("tensor", None, None),
        P("dp", ("context", "tensor"), None),
    )
    return jax.shard_map(
        shards,
        mesh=mesh,
        in_specs=placed,
        out_specs=(
            P("dp", ("context", "tensor"), None),
            P("dp", ("context", "tensor"), None),
            P(("context", "tensor"), None),
            P("tensor", None, None),
            P("tensor", None, None),
            P("tensor", None, None),
            P("tensor", None, None),
        ),
        check_vma=False,
    )
```

```python
import math

import jax
import jax.numpy as jnp
from jax import lax
from jax.sharding import PartitionSpec as P

table_mode = lax.Precision.DEFAULT


def blockwise(acts, weight):
    rows = acts.shape[0]
    shaped = acts.reshape(rows, weight.shape[0], weight.shape[1])
    return jnp.einsum("tni,nij->tnj", shaped, weight, preferred_element_type=jnp.float32).reshape(
        rows, -1
    )


def blockwise_back(acts, weight):
    rows = acts.shape[0]
    shaped = acts.reshape(rows, weight.shape[0], weight.shape[1])
    return jnp.einsum("tnj,nij->tni", shaped, weight, preferred_element_type=jnp.float32).reshape(
        rows, -1
    )


def weight_term(inputs, grads, blocks):
    rows = inputs.shape[0]
    left = inputs.reshape(rows, blocks, -1)
    right = grads.reshape(rows, blocks, -1)
    return jnp.einsum("tni,tnj->nij", left, right, preferred_element_type=jnp.float32)


def angle_table(rows, cols, total):
    product = (
        jnp.arange(rows, dtype=jnp.int32)[:, None]
        * jnp.arange(cols, dtype=jnp.int32)[None, :]
        % total
    )
    angle = product.astype(jnp.float32) * (2.0 * math.pi / total)
    return (jnp.cos(angle), jnp.sin(angle))


def make_tables(length):
    second = length // 128
    cosine_first, sine_first = angle_table(128, 128, 128)
    cosine_second, sine_second = angle_table(second, second, second)
    cosine_twist, sine_twist = angle_table(128, second, length)
    return (
        cosine_first,
        sine_first,
        cosine_second,
        sine_second,
        cosine_twist[:, :, None],
        sine_twist[:, :, None],
    )


def across_first(matrix, array):
    return jnp.einsum(
        "kn,nmc->kmc", matrix, array, precision=table_mode, preferred_element_type=jnp.float32
    )


def across_second(array, matrix):
    return jnp.einsum(
        "kmc,ml->klc", array, matrix, precision=table_mode, preferred_element_type=jnp.float32
    )


def forward_transform(signal, tables):
    cosine_first, sine_first, cosine_second, sine_second, cosine_twist, sine_twist = tables
    half = cosine_first.shape[0] // 2
    shaped = signal.reshape(half, cosine_second.shape[0], signal.shape[1])
    real_section = across_first(cosine_first[:, :half], shaped)
    imag_section = -across_first(sine_first[:, :half], shaped)
    real_turned = real_section * cosine_twist + imag_section * sine_twist
    imag_turned = imag_section * cosine_twist - real_section * sine_twist
    real_out = across_second(real_turned, cosine_second) + across_second(imag_turned, sine_second)
    imag_out = across_second(imag_turned, cosine_second) - across_second(real_turned, sine_second)
    return (real_out, imag_out)


def inverse_transform(real_spec, imag_spec, tables):
    cosine_first, sine_first, cosine_second, sine_second, cosine_twist, sine_twist = tables
    half = cosine_first.shape[0] // 2
    total = cosine_first.shape[0] * cosine_second.shape[0]
    real_section = across_second(real_spec, cosine_second) - across_second(imag_spec, sine_second)
    imag_section = across_second(imag_spec, cosine_second) + across_second(real_spec, sine_second)
    real_turned = real_section * cosine_twist - imag_section * sine_twist
    imag_turned = imag_section * cosine_twist + real_section * sine_twist
    signal = (
        across_first(cosine_first[:half], real_turned)
        - across_first(sine_first[:half], imag_turned)
    ) / total
    return signal.reshape(half * cosine_second.shape[0], -1)


def spectral_tables(length):
    first = 128
    second = length // first
    half = first // 2
    cosine_first, sine_first = angle_table(first, first, first)
    cosine_second, sine_second = angle_table(second, second, second)
    cosine_twist, sine_twist = angle_table(first, second, length)
    forward_first = jnp.concatenate([cosine_first[:, :half], -sine_first[:, :half]], axis=0)
    forward_second = jnp.stack(
        [
            jnp.stack([cosine_second, -sine_second], axis=1),
            jnp.stack([sine_second, cosine_second], axis=1),
        ]
    )
    inverse_second = jnp.stack(
        [
            jnp.stack([cosine_second, sine_second], axis=1),
            jnp.stack([-sine_second, cosine_second], axis=1),
        ]
    )
    inverse_first = jnp.stack([cosine_first[:half], -sine_first[:half]], axis=1) / length
    return (
        forward_first,
        forward_second,
        inverse_second,
        inverse_first,
        cosine_twist[:, :, None],
        sine_twist[:, :, None],
    )


def spectra(signal, tables):
    forward_first, forward_second, _, _, cosine_twist, sine_twist = tables
    first = cosine_twist.shape[0]
    half = first // 2
    shaped = signal.reshape(half, cosine_twist.shape[1], signal.shape[1])
    section = jnp.einsum(
        "kn,nmc->kmc", forward_first, shaped, precision=table_mode,
        preferred_element_type=jnp.float32,
    )
    real_section, imag_section = section[:first], section[first:]
    turned = jnp.stack(
        [
            real_section * cosine_twist + imag_section * sine_twist,
            imag_section * cosine_twist - real_section * sine_twist,
        ]
    )
    return jnp.einsum(
        "rkmc,rmsl->sklc", turned, forward_second, precision=table_mode,
        preferred_element_type=jnp.float32,
    )


def signals(spec, tables):
    _, _, inverse_second, inverse_first, cosine_twist, sine_twist = tables
    section = jnp.einsum(
        "sklc,slrm->rkmc", spec, inverse_second, precision=table_mode,
        preferred_element_type=jnp.float32,
    )
    real_section, imag_section = section[0], section[1]
    turned = jnp.stack(
        [
            real_section * cosine_twist - imag_section * sine_twist,
            imag_section * cosine_twist + real_section * sine_twist,
        ]
    )
    out = jnp.einsum(
        "nrk,rkmc->nmc", inverse_first, turned, precision=table_mode,
        preferred_element_type=jnp.float32,
    )
    return out.reshape(-1, out.shape[-1])


def shards(
    tokens, filter_taps, query_weight, key_weight, value_weight, output_weight, out_cotangent
):
    ctx = lax.axis_size("context")
    ten = lax.axis_size("tensor")
    rows = tokens.shape[1]
    arrived = lax.all_to_all(
        jnp.concatenate(
            [tokens[0], out_cotangent[0], filter_taps.astype(jnp.bfloat16)], axis=0
        ),
        "tensor",
        split_axis=1,
        concat_axis=0,
        tiled=True,
    )
    arrived = arrived.reshape(ten, 3, rows, arrived.shape[1])
    inputs = arrived[:, 0].reshape(ten * rows, -1)
    upstream = arrived[:, 1].reshape(ten * rows, -1)
    taps_mid = arrived[:, 2].reshape(ten * rows, -1)
    blocks = query_weight.shape[0]
    query = blockwise(inputs, query_weight).astype(jnp.bfloat16)
    keys = blockwise(inputs, key_weight).astype(jnp.bfloat16)
    values = blockwise(inputs, value_weight).astype(jnp.bfloat16)
    gated = (keys.astype(jnp.float32) * values.astype(jnp.float32)).astype(jnp.bfloat16)
    query_wide = query.astype(jnp.float32)
    back_weighted = blockwise_back(upstream, output_weight)
    conv_grad = (back_weighted * query_wide).astype(jnp.bfloat16)
    local = inputs.shape[0]
    gated_time, grad_time, taps = (
        lax.all_to_all(part, "context", split_axis=1, concat_axis=0, tiled=True)
        for part in (gated, conv_grad, taps_mid)
    )
    taps = taps.astype(jnp.float32)
    length = taps.shape[0]
    width = taps.shape[1]
    tables = spectral_tables(2 * length)
    spec = spectra(
        jnp.concatenate(
            [taps, gated_time.astype(jnp.float32), grad_time.astype(jnp.float32)], axis=1
        ),
        tables,
    )
    real_spec, imag_spec = spec[0], spec[1]
    real_taps, real_gated, real_grad = (
        real_spec[..., :width], real_spec[..., width : 2 * width], real_spec[..., 2 * width :]
    )
    imag_taps, imag_gated, imag_grad = (
        imag_spec[..., :width], imag_spec[..., width : 2 * width], imag_spec[..., 2 * width :]
    )
    products = jnp.stack(
        [
            jnp.concatenate(
                [
                    real_taps * real_gated - imag_taps * imag_gated,
                    real_taps * real_grad + imag_taps * imag_grad,
                    real_grad * real_gated + imag_grad * imag_gated,
                ],
                axis=-1,
            ),
            jnp.concatenate(
                [
                    real_taps * imag_gated + imag_taps * real_gated,
                    real_taps * imag_grad - imag_taps * real_grad,
                    imag_grad * real_gated - real_grad * imag_gated,
                ],
                axis=-1,
            ),
        ]
    )
    results = signals(products, tables)
    conv_time = results[:, :width]
    gated_time_back = results[:, width : 2 * width]
    taps_back = results[:, 2 * width :]
    returned = lax.all_to_all(
        jnp.stack(
            [
                conv_time.astype(jnp.bfloat16).reshape(ctx, local, width),
                gated_time_back.astype(jnp.bfloat16).reshape(ctx, local, width),
            ],
            axis=1,
        ).reshape(ctx * 2 * local, width),
        "context",
        split_axis=0,
        concat_axis=1,
        tiled=True,
    )
    conv, gated_narrow = returned[:local], returned[local:]
    conv_wide = conv.astype(jnp.float32)
    weighted = (query_wide * conv_wide).astype(jnp.bfloat16)
    query_back = (back_weighted * conv_wide).astype(jnp.bfloat16)
    gated_back = gated_narrow.astype(jnp.float32)
    key_back = (gated_back * values.astype(jnp.float32)).astype(jnp.bfloat16)
    value_back = (gated_back * keys.astype(jnp.float32)).astype(jnp.bfloat16)
    factor = 1.0 / math.sqrt(lax.axis_size("dp") * length)
    terms = (
        (weight_term(inputs, query_back, blocks) * factor).astype(jnp.bfloat16),
        (weight_term(inputs, key_back, blocks) * factor).astype(jnp.bfloat16),
        (weight_term(inputs, value_back, blocks) * factor).astype(jnp.bfloat16),
        (weight_term(weighted, upstream, blocks) * factor).astype(jnp.bfloat16),
    )
    terms, (query_back, key_back, value_back, weighted) = lax.optimization_barrier(
        (terms, (query_back, key_back, value_back, weighted))
    )
    query_grad, key_grad, value_grad, output_grad = (
        lax.psum(term, ("dp", "context")).astype(jnp.float32) for term in terms
    )
    mixed = blockwise(weighted, output_weight).astype(jnp.bfloat16)
    token_grad = (
        blockwise_back(query_back, query_weight)
        + blockwise_back(key_back, key_weight)
        + blockwise_back(value_back, value_weight)
    ).astype(jnp.bfloat16)
    taps_total = lax.psum((taps_back * factor).astype(jnp.bfloat16), "dp")
    filter_mid = lax.all_to_all(taps_total, "context", split_axis=0, concat_axis=1, tiled=True)
    leaving = lax.all_to_all(
        jnp.stack(
            [
                part.reshape(ten, rows, part.shape[1])
                for part in (mixed, token_grad, filter_mid)
            ],
            axis=1,
        ).reshape(ten * 3 * rows, -1),
        "tensor",
        split_axis=0,
        concat_axis=1,
        tiled=True,
    )
    mixed_rows = leaving[:rows]
    grad_rows = leaving[rows : 2 * rows]
    filter_grad = leaving[2 * rows :].astype(jnp.float32)
    return (
        mixed_rows[None],
        grad_rows[None],
        filter_grad,
        query_grad,
        key_grad,
        value_grad,
        output_grad,
    )


def solution(mesh):
    placed = (
        P("dp", ("context", "tensor"), None),
        P(("context", "tensor"), None),
        P("tensor", None, None),
        P("tensor", None, None),
        P("tensor", None, None),
        P("tensor", None, None),
        P("dp", ("context", "tensor"), None),
    )
    return jax.shard_map(
        shards,
        mesh=mesh,
        in_specs=placed,
        out_specs=(
            P("dp", ("context", "tensor"), None),
            P("dp", ("context", "tensor"), None),
            P(("context", "tensor"), None),
            P("tensor", None, None),
            P("tensor", None, None),
            P("tensor", None, None),
            P("tensor", None, None),
        ),
        check_vma=False,
    )
```

```python
import math

import jax
import jax.numpy as jnp
from jax import lax
from jax.sharding import PartitionSpec as P

table_mode = lax.Precision.DEFAULT


def blockwise(acts, weight):
    rows = acts.shape[0]
    shaped = acts.reshape(rows, weight.shape[0], weight.shape[1])
    return jnp.einsum("tni,nij->tnj", shaped, weight, preferred_element_type=jnp.float32).reshape(
        rows, -1
    )


def blockwise_back(acts, weight):
    rows = acts.shape[0]
    shaped = acts.reshape(rows, weight.shape[0], weight.shape[1])
    return jnp.einsum("tnj,nij->tni", shaped, weight, preferred_element_type=jnp.float32).reshape(
        rows, -1
    )


def weight_term(inputs, grads, blocks):
    rows = inputs.shape[0]
    left = inputs.reshape(rows, blocks, -1)
    right = grads.reshape(rows, blocks, -1)
    return jnp.einsum("tni,tnj->nij", left, right, preferred_element_type=jnp.float32)


def angle_table(rows, cols, total):
    product = (
        jnp.arange(rows, dtype=jnp.int32)[:, None]
        * jnp.arange(cols, dtype=jnp.int32)[None, :]
        % total
    )
    angle = product.astype(jnp.float32) * (2.0 * math.pi / total)
    return (jnp.cos(angle), jnp.sin(angle))


def make_tables(length):
    second = length // 128
    cosine_first, sine_first = angle_table(128, 128, 128)
    cosine_second, sine_second = angle_table(second, second, second)
    cosine_twist, sine_twist = angle_table(128, second, length)
    return (
        cosine_first,
        sine_first,
        cosine_second,
        sine_second,
        cosine_twist[:, :, None],
        sine_twist[:, :, None],
    )


def across_first(matrix, array):
    return jnp.einsum(
        "kn,nmc->kmc", matrix, array, precision=table_mode, preferred_element_type=jnp.float32
    )


def across_second(array, matrix):
    return jnp.einsum(
        "kmc,ml->klc", array, matrix, precision=table_mode, preferred_element_type=jnp.float32
    )


def forward_transform(signal, tables):
    cosine_first, sine_first, cosine_second, sine_second, cosine_twist, sine_twist = tables
    half = cosine_first.shape[0] // 2
    shaped = signal.reshape(half, cosine_second.shape[0], signal.shape[1])
    real_section = across_first(cosine_first[:, :half], shaped)
    imag_section = -across_first(sine_first[:, :half], shaped)
    real_turned = real_section * cosine_twist + imag_section * sine_twist
    imag_turned = imag_section * cosine_twist - real_section * sine_twist
    real_out = across_second(real_turned, cosine_second) + across_second(imag_turned, sine_second)
    imag_out = across_second(imag_turned, cosine_second) - across_second(real_turned, sine_second)
    return (real_out, imag_out)


def inverse_transform(real_spec, imag_spec, tables):
    cosine_first, sine_first, cosine_second, sine_second, cosine_twist, sine_twist = tables
    half = cosine_first.shape[0] // 2
    total = cosine_first.shape[0] * cosine_second.shape[0]
    real_section = across_second(real_spec, cosine_second) - across_second(imag_spec, sine_second)
    imag_section = across_second(imag_spec, cosine_second) + across_second(real_spec, sine_second)
    real_turned = real_section * cosine_twist - imag_section * sine_twist
    imag_turned = imag_section * cosine_twist + real_section * sine_twist
    signal = (
        across_first(cosine_first[:half], real_turned)
        - across_first(sine_first[:half], imag_turned)
    ) / total
    return signal.reshape(half * cosine_second.shape[0], -1)


def spectral_tables(length):
    first = 128
    second = length // first
    half = first // 2
    cosine_first, sine_first = angle_table(first, first, first)
    cosine_second, sine_second = angle_table(second, second, second)
    cosine_twist, sine_twist = angle_table(first, second, length)
    forward_first = jnp.concatenate([cosine_first[:, :half], -sine_first[:, :half]], axis=0)
    forward_second = jnp.stack(
        [
            jnp.stack([cosine_second, -sine_second], axis=1),
            jnp.stack([sine_second, cosine_second], axis=1),
        ]
    )
    inverse_second = jnp.stack(
        [
            jnp.stack([cosine_second, sine_second], axis=1),
            jnp.stack([-sine_second, cosine_second], axis=1),
        ]
    )
    inverse_first = jnp.stack([cosine_first[:half], -sine_first[:half]], axis=1) / length
    return (
        forward_first,
        forward_second,
        inverse_second,
        inverse_first,
        cosine_twist[:, :, None],
        sine_twist[:, :, None],
    )


def spectra(signal, tables):
    forward_first, forward_second, _, _, cosine_twist, sine_twist = tables
    first = cosine_twist.shape[0]
    half = first // 2
    shaped = signal.reshape(half, cosine_twist.shape[1], signal.shape[1])
    section = jnp.einsum(
        "kn,nmc->kmc", forward_first, shaped, precision=table_mode,
        preferred_element_type=jnp.float32,
    )
    real_section, imag_section = section[:first], section[first:]
    turned = jnp.stack(
        [
            real_section * cosine_twist + imag_section * sine_twist,
            imag_section * cosine_twist - real_section * sine_twist,
        ]
    )
    return tuple(
        jnp.einsum(
            "rkmc,rml->klc", turned, forward_second[:, :, part], precision=table_mode,
            preferred_element_type=jnp.float32,
        )
        for part in range(2)
    )


def signals(spec, tables):
    _, _, inverse_second, inverse_first, cosine_twist, sine_twist = tables
    section = jnp.einsum(
        "sklc,slrm->rkmc", spec, inverse_second, precision=table_mode,
        preferred_element_type=jnp.float32,
    )
    real_section, imag_section = section[0], section[1]
    turned = jnp.stack(
        [
            real_section * cosine_twist - imag_section * sine_twist,
            imag_section * cosine_twist + real_section * sine_twist,
        ]
    )
    out = jnp.einsum(
        "nrk,rkmc->nmc", inverse_first, turned, precision=table_mode,
        preferred_element_type=jnp.float32,
    )
    return out.reshape(-1, out.shape[-1])


def shards(
    tokens, filter_taps, query_weight, key_weight, value_weight, output_weight, out_cotangent
):
    ctx = lax.axis_size("context")
    ten = lax.axis_size("tensor")
    rows = tokens.shape[1]
    arrived = lax.all_to_all(
        jnp.concatenate(
            [tokens[0], out_cotangent[0], filter_taps.astype(jnp.bfloat16)], axis=0
        ),
        "tensor",
        split_axis=1,
        concat_axis=0,
        tiled=True,
    )
    arrived = arrived.reshape(ten, 3, rows, arrived.shape[1])
    inputs = arrived[:, 0].reshape(ten * rows, -1)
    upstream = arrived[:, 1].reshape(ten * rows, -1)
    taps_mid = arrived[:, 2].reshape(ten * rows, -1)
    blocks = query_weight.shape[0]
    query = blockwise(inputs, query_weight).astype(jnp.bfloat16)
    keys = blockwise(inputs, key_weight).astype(jnp.bfloat16)
    values = blockwise(inputs, value_weight).astype(jnp.bfloat16)
    gated = (keys.astype(jnp.float32) * values.astype(jnp.float32)).astype(jnp.bfloat16)
    query_wide = query.astype(jnp.float32)
    back_weighted = blockwise_back(upstream, output_weight)
    conv_grad = (back_weighted * query_wide).astype(jnp.bfloat16)
    local = inputs.shape[0]
    gated_time, grad_time, taps = (
        lax.all_to_all(part, "context", split_axis=1, concat_axis=0, tiled=True)
        for part in (gated, conv_grad, taps_mid)
    )
    taps = taps.astype(jnp.float32)
    length = taps.shape[0]
    width = taps.shape[1]
    tables = spectral_tables(2 * length)
    spec = spectra(
        jnp.concatenate(
            [taps, gated_time.astype(jnp.float32), grad_time.astype(jnp.float32)], axis=1
        ),
        tables,
    )
    real_spec, imag_spec = spec
    real_taps, real_gated, real_grad = (
        real_spec[..., :width], real_spec[..., width : 2 * width], real_spec[..., 2 * width :]
    )
    imag_taps, imag_gated, imag_grad = (
        imag_spec[..., :width], imag_spec[..., width : 2 * width], imag_spec[..., 2 * width :]
    )
    products = jnp.stack(
        [
            jnp.concatenate(
                [
                    real_taps * real_gated - imag_taps * imag_gated,
                    real_taps * real_grad + imag_taps * imag_grad,
                    real_grad * real_gated + imag_grad * imag_gated,
                ],
                axis=-1,
            ),
            jnp.concatenate(
                [
                    real_taps * imag_gated + imag_taps * real_gated,
                    real_taps * imag_grad - imag_taps * real_grad,
                    imag_grad * real_gated - real_grad * imag_gated,
                ],
                axis=-1,
            ),
        ]
    )
    results = signals(products, tables)
    conv_time = results[:, :width]
    gated_time_back = results[:, width : 2 * width]
    taps_back = results[:, 2 * width :]
    returned = lax.all_to_all(
        jnp.stack(
            [
                conv_time.astype(jnp.bfloat16).reshape(ctx, local, width),
                gated_time_back.astype(jnp.bfloat16).reshape(ctx, local, width),
            ],
            axis=1,
        ).reshape(ctx * 2 * local, width),
        "context",
        split_axis=0,
        concat_axis=1,
        tiled=True,
    )
    conv, gated_narrow = returned[:local], returned[local:]
    conv_wide = conv.astype(jnp.float32)
    weighted = (query_wide * conv_wide).astype(jnp.bfloat16)
    query_back = (back_weighted * conv_wide).astype(jnp.bfloat16)
    gated_back = gated_narrow.astype(jnp.float32)
    key_back = (gated_back * values.astype(jnp.float32)).astype(jnp.bfloat16)
    value_back = (gated_back * keys.astype(jnp.float32)).astype(jnp.bfloat16)
    factor = 1.0 / math.sqrt(lax.axis_size("dp") * length)
    terms = (
        (weight_term(inputs, query_back, blocks) * factor).astype(jnp.bfloat16),
        (weight_term(inputs, key_back, blocks) * factor).astype(jnp.bfloat16),
        (weight_term(inputs, value_back, blocks) * factor).astype(jnp.bfloat16),
        (weight_term(weighted, upstream, blocks) * factor).astype(jnp.bfloat16),
    )
    terms, (query_back, key_back, value_back, weighted) = lax.optimization_barrier(
        (terms, (query_back, key_back, value_back, weighted))
    )
    query_grad, key_grad, value_grad, output_grad = (
        lax.psum(term, ("dp", "context")).astype(jnp.float32) for term in terms
    )
    mixed = blockwise(weighted, output_weight).astype(jnp.bfloat16)
    token_grad = (
        blockwise_back(query_back, query_weight)
        + blockwise_back(key_back, key_weight)
        + blockwise_back(value_back, value_weight)
    ).astype(jnp.bfloat16)
    taps_total = lax.psum((taps_back * factor).astype(jnp.bfloat16), "dp")
    filter_mid = lax.all_to_all(taps_total, "context", split_axis=0, concat_axis=1, tiled=True)
    leaving = lax.all_to_all(
        jnp.stack(
            [
                part.reshape(ten, rows, part.shape[1])
                for part in (mixed, token_grad, filter_mid)
            ],
            axis=1,
        ).reshape(ten * 3 * rows, -1),
        "tensor",
        split_axis=0,
        concat_axis=1,
        tiled=True,
    )
    mixed_rows = leaving[:rows]
    grad_rows = leaving[rows : 2 * rows]
    filter_grad = leaving[2 * rows :].astype(jnp.float32)
    return (
        mixed_rows[None],
        grad_rows[None],
        filter_grad,
        query_grad,
        key_grad,
        value_grad,
        output_grad,
    )


def solution(mesh):
    placed = (
        P("dp", ("context", "tensor"), None),
        P(("context", "tensor"), None),
        P("tensor", None, None),
        P("tensor", None, None),
        P("tensor", None, None),
        P("tensor", None, None),
        P("dp", ("context", "tensor"), None),
    )
    return jax.shard_map(
        shards,
        mesh=mesh,
        in_specs=placed,
        out_specs=(
            P("dp", ("context", "tensor"), None),
            P("dp", ("context", "tensor"), None),
            P(("context", "tensor"), None),
            P("tensor", None, None),
            P("tensor", None, None),
            P("tensor", None, None),
            P("tensor", None, None),
        ),
        check_vma=False,
    )
```

```python
import math

import jax
import jax.numpy as jnp
from jax import lax
from jax.sharding import PartitionSpec as P

table_mode = lax.Precision.DEFAULT


def blockwise(acts, weight):
    rows = acts.shape[0]
    shaped = acts.reshape(rows, weight.shape[0], weight.shape[1])
    return jnp.einsum("tni,nij->tnj", shaped, weight, preferred_element_type=jnp.float32).reshape(
        rows, -1
    )


def blockwise_back(acts, weight):
    rows = acts.shape[0]
    shaped = acts.reshape(rows, weight.shape[0], weight.shape[1])
    return jnp.einsum("tnj,nij->tni", shaped, weight, preferred_element_type=jnp.float32).reshape(
        rows, -1
    )


def weight_term(inputs, grads, blocks):
    rows = inputs.shape[0]
    left = inputs.reshape(rows, blocks, -1)
    right = grads.reshape(rows, blocks, -1)
    return jnp.einsum("tni,tnj->nij", left, right, preferred_element_type=jnp.float32)


def angle_table(rows, cols, total):
    product = (
        jnp.arange(rows, dtype=jnp.int32)[:, None]
        * jnp.arange(cols, dtype=jnp.int32)[None, :]
        % total
    )
    angle = product.astype(jnp.float32) * (2.0 * math.pi / total)
    return (jnp.cos(angle), jnp.sin(angle))


def make_tables(length):
    second = length // 128
    cosine_first, sine_first = angle_table(128, 128, 128)
    cosine_second, sine_second = angle_table(second, second, second)
    cosine_twist, sine_twist = angle_table(128, second, length)
    return (
        cosine_first,
        sine_first,
        cosine_second,
        sine_second,
        cosine_twist[:, :, None],
        sine_twist[:, :, None],
    )


def across_first(matrix, array):
    return jnp.einsum(
        "kn,nmc->kmc", matrix, array, precision=table_mode, preferred_element_type=jnp.float32
    )


def across_second(array, matrix):
    return jnp.einsum(
        "kmc,ml->klc", array, matrix, precision=table_mode, preferred_element_type=jnp.float32
    )


def forward_transform(signal, tables):
    cosine_first, sine_first, cosine_second, sine_second, cosine_twist, sine_twist = tables
    half = cosine_first.shape[0] // 2
    shaped = signal.reshape(half, cosine_second.shape[0], signal.shape[1])
    real_section = across_first(cosine_first[:, :half], shaped)
    imag_section = -across_first(sine_first[:, :half], shaped)
    real_turned = real_section * cosine_twist + imag_section * sine_twist
    imag_turned = imag_section * cosine_twist - real_section * sine_twist
    real_out = across_second(real_turned, cosine_second) + across_second(imag_turned, sine_second)
    imag_out = across_second(imag_turned, cosine_second) - across_second(real_turned, sine_second)
    return (real_out, imag_out)


def inverse_transform(real_spec, imag_spec, tables):
    cosine_first, sine_first, cosine_second, sine_second, cosine_twist, sine_twist = tables
    half = cosine_first.shape[0] // 2
    total = cosine_first.shape[0] * cosine_second.shape[0]
    real_section = across_second(real_spec, cosine_second) - across_second(imag_spec, sine_second)
    imag_section = across_second(imag_spec, cosine_second) + across_second(real_spec, sine_second)
    real_turned = real_section * cosine_twist - imag_section * sine_twist
    imag_turned = imag_section * cosine_twist + real_section * sine_twist
    signal = (
        across_first(cosine_first[:half], real_turned)
        - across_first(sine_first[:half], imag_turned)
    ) / total
    return signal.reshape(half * cosine_second.shape[0], -1)


def spectral_tables(length):
    first = 128
    second = length // first
    half = first // 2
    cosine_first, sine_first = angle_table(first, first, first)
    cosine_second, sine_second = angle_table(second, second, second)
    cosine_twist, sine_twist = angle_table(first, second, length)
    forward_first = jnp.concatenate([cosine_first[:, :half], -sine_first[:, :half]], axis=0)
    forward_second = jnp.stack(
        [
            jnp.stack([cosine_second, -sine_second], axis=1),
            jnp.stack([sine_second, cosine_second], axis=1),
        ]
    )
    inverse_second = jnp.stack(
        [
            jnp.stack([cosine_second, sine_second], axis=1),
            jnp.stack([-sine_second, cosine_second], axis=1),
        ]
    )
    inverse_first = jnp.stack([cosine_first[:half], -sine_first[:half]], axis=1) / length
    return (
        forward_first,
        forward_second,
        inverse_second,
        inverse_first,
        cosine_twist[:, :, None],
        sine_twist[:, :, None],
    )


def spectra(signal, tables):
    forward_first, forward_second, _, _, cosine_twist, sine_twist = tables
    first = cosine_twist.shape[0]
    half = first // 2
    shaped = signal.reshape(half, cosine_twist.shape[1], signal.shape[1])
    section = jnp.einsum(
        "kn,nmc->kmc", forward_first, shaped, precision=table_mode,
        preferred_element_type=jnp.float32,
    )
    real_section, imag_section = section[:first], section[first:]
    turned = jnp.stack(
        [
            real_section * cosine_twist + imag_section * sine_twist,
            imag_section * cosine_twist - real_section * sine_twist,
        ]
    )
    return tuple(
        jnp.einsum(
            "rkmc,rml->klc", turned, forward_second[:, :, part], precision=table_mode,
            preferred_element_type=jnp.float32,
        )
        for part in range(2)
    )


def signals(spec, tables):
    _, _, inverse_second, inverse_first, cosine_twist, sine_twist = tables
    section = jnp.einsum(
        "sklc,slrm->rkmc", spec, inverse_second, precision=table_mode,
        preferred_element_type=jnp.float32,
    )
    real_section, imag_section = section[0], section[1]
    turned = jnp.stack(
        [
            real_section * cosine_twist - imag_section * sine_twist,
            imag_section * cosine_twist + real_section * sine_twist,
        ]
    )
    out = jnp.einsum(
        "nrk,rkmc->nmc", inverse_first, turned, precision=table_mode,
        preferred_element_type=jnp.float32,
    )
    return out.reshape(-1, out.shape[-1])


def shards(
    tokens, filter_taps, query_weight, key_weight, value_weight, output_weight, out_cotangent
):
    ctx = lax.axis_size("context")
    ten = lax.axis_size("tensor")
    rows = tokens.shape[1]
    arrived = lax.all_to_all(
        jnp.concatenate(
            [tokens[0], out_cotangent[0], filter_taps.astype(jnp.bfloat16)], axis=0
        ),
        "tensor",
        split_axis=1,
        concat_axis=0,
        tiled=True,
    )
    arrived = arrived.reshape(ten, 3, rows, arrived.shape[1])
    inputs = arrived[:, 0].reshape(ten * rows, -1)
    upstream = arrived[:, 1].reshape(ten * rows, -1)
    taps_mid = arrived[:, 2].reshape(ten * rows, -1)
    blocks = query_weight.shape[0]
    query = blockwise(inputs, query_weight).astype(jnp.bfloat16)
    keys = blockwise(inputs, key_weight).astype(jnp.bfloat16)
    values = blockwise(inputs, value_weight).astype(jnp.bfloat16)
    gated = (keys.astype(jnp.float32) * values.astype(jnp.float32)).astype(jnp.bfloat16)
    query_wide = query.astype(jnp.float32)
    back_weighted = blockwise_back(upstream, output_weight)
    conv_grad = (back_weighted * query_wide).astype(jnp.bfloat16)
    local = inputs.shape[0]
    gated_time, grad_time, taps = (
        lax.all_to_all(part, "context", split_axis=1, concat_axis=0, tiled=True)
        for part in (gated, conv_grad, taps_mid)
    )
    taps = taps.astype(jnp.float32)
    length = taps.shape[0]
    width = taps.shape[1]
    tables = spectral_tables(2 * length)
    spec = spectra(
        jnp.concatenate(
            [taps, gated_time.astype(jnp.float32), grad_time.astype(jnp.float32)], axis=1
        ),
        tables,
    )
    real_spec, imag_spec = spec
    real_taps, real_gated, real_grad = (
        real_spec[..., :width], real_spec[..., width : 2 * width], real_spec[..., 2 * width :]
    )
    imag_taps, imag_gated, imag_grad = (
        imag_spec[..., :width], imag_spec[..., width : 2 * width], imag_spec[..., 2 * width :]
    )
    products = jnp.stack(
        [
            jnp.concatenate(
                [
                    real_taps * real_gated - imag_taps * imag_gated,
                    real_taps * real_grad + imag_taps * imag_grad,
                    real_grad * real_gated + imag_grad * imag_gated,
                ],
                axis=-1,
            ),
            jnp.concatenate(
                [
                    real_taps * imag_gated + imag_taps * real_gated,
                    real_taps * imag_grad - imag_taps * real_grad,
                    imag_grad * real_gated - real_grad * imag_gated,
                ],
                axis=-1,
            ),
        ]
    )
    results = signals(products, tables)
    conv_time = results[:, :width]
    gated_time_back = results[:, width : 2 * width]
    taps_back = results[:, 2 * width :]
    returned = lax.all_to_all(
        jnp.stack(
            [
                conv_time.astype(jnp.bfloat16).reshape(ctx, local, width),
                gated_time_back.astype(jnp.bfloat16).reshape(ctx, local, width),
            ],
            axis=1,
        ).reshape(ctx * 2 * local, width),
        "context",
        split_axis=0,
        concat_axis=1,
        tiled=True,
    )
    conv, gated_narrow = returned[:local], returned[local:]
    conv_wide = conv.astype(jnp.float32)
    weighted = (query_wide * conv_wide).astype(jnp.bfloat16)
    query_back = (back_weighted * conv_wide).astype(jnp.bfloat16)
    gated_back = gated_narrow.astype(jnp.float32)
    key_back = (gated_back * values.astype(jnp.float32)).astype(jnp.bfloat16)
    value_back = (gated_back * keys.astype(jnp.float32)).astype(jnp.bfloat16)
    factor = 1.0 / math.sqrt(lax.axis_size("dp") * length)
    terms = (
        (weight_term(inputs, query_back, blocks) * factor).astype(jnp.bfloat16),
        (weight_term(inputs, key_back, blocks) * factor).astype(jnp.bfloat16),
        (weight_term(inputs, value_back, blocks) * factor).astype(jnp.bfloat16),
        (weight_term(weighted, upstream, blocks) * factor).astype(jnp.bfloat16),
    )
    terms, (query_back, key_back, value_back, weighted) = lax.optimization_barrier(
        (terms, (query_back, key_back, value_back, weighted))
    )
    pair = lax.axis_index("dp")
    swap = [(0, 1), (1, 0)]
    flat = lax.optimization_barrier(
        jnp.concatenate([term.reshape(2, -1) for term in terms], axis=1)
    )
    kept = lax.dynamic_index_in_dim(flat, pair, axis=0, keepdims=False)
    given = lax.dynamic_index_in_dim(flat, 1 - pair, axis=0, keepdims=False)
    taken = lax.ppermute(given, "dp", swap)
    half = (kept.astype(jnp.float32) + taken.astype(jnp.float32)).astype(jnp.bfloat16)
    half = lax.psum(half, "context")
    other = lax.ppermute(half, "dp", swap)
    span = half.shape[0]
    whole = lax.dynamic_slice_in_dim(
        jnp.concatenate([half, other, half]), pair * span, 2 * span
    ).reshape(2, span)
    share = span // len(terms)
    query_grad, key_grad, value_grad, output_grad = (
        whole[:, index * share : (index + 1) * share]
        .reshape(terms[index].shape)
        .astype(jnp.float32)
        for index in range(len(terms))
    )
    mixed = blockwise(weighted, output_weight).astype(jnp.bfloat16)
    token_grad = (
        blockwise_back(query_back, query_weight)
        + blockwise_back(key_back, key_weight)
        + blockwise_back(value_back, value_weight)
    ).astype(jnp.bfloat16)
    taps_total = lax.psum((taps_back * factor).astype(jnp.bfloat16), "dp")
    filter_mid = lax.all_to_all(taps_total, "context", split_axis=0, concat_axis=1, tiled=True)
    leaving = lax.all_to_all(
        jnp.stack(
            [
                part.reshape(ten, rows, part.shape[1])
                for part in (mixed, token_grad, filter_mid)
            ],
            axis=1,
        ).reshape(ten * 3 * rows, -1),
        "tensor",
        split_axis=0,
        concat_axis=1,
        tiled=True,
    )
    mixed_rows = leaving[:rows]
    grad_rows = leaving[rows : 2 * rows]
    filter_grad = leaving[2 * rows :].astype(jnp.float32)
    return (
        mixed_rows[None],
        grad_rows[None],
        filter_grad,
        query_grad,
        key_grad,
        value_grad,
        output_grad,
    )


def solution(mesh):
    placed = (
        P("dp", ("context", "tensor"), None),
        P(("context", "tensor"), None),
        P("tensor", None, None),
        P("tensor", None, None),
        P("tensor", None, None),
        P("tensor", None, None),
        P("dp", ("context", "tensor"), None),
    )
    return jax.shard_map(
        shards,
        mesh=mesh,
        in_specs=placed,
        out_specs=(
            P("dp", ("context", "tensor"), None),
            P("dp", ("context", "tensor"), None),
            P(("context", "tensor"), None),
            P("tensor", None, None),
            P("tensor", None, None),
            P("tensor", None, None),
            P("tensor", None, None),
        ),
        check_vma=False,
    )
```

```python
import math

import jax
import jax.numpy as jnp
from jax import lax
from jax.sharding import PartitionSpec as P

table_mode = lax.Precision.DEFAULT


def blockwise(acts, weight):
    rows = acts.shape[0]
    shaped = acts.reshape(rows, weight.shape[0], weight.shape[1])
    return jnp.einsum("tni,nij->tnj", shaped, weight, preferred_element_type=jnp.float32).reshape(
        rows, -1
    )


def blockwise_back(acts, weight):
    rows = acts.shape[0]
    shaped = acts.reshape(rows, weight.shape[0], weight.shape[1])
    return jnp.einsum("tnj,nij->tni", shaped, weight, preferred_element_type=jnp.float32).reshape(
        rows, -1
    )


def weight_term(inputs, grads, blocks):
    rows = inputs.shape[0]
    left = inputs.reshape(rows, blocks, -1)
    right = grads.reshape(rows, blocks, -1)
    return jnp.einsum("tni,tnj->nij", left, right, preferred_element_type=jnp.float32)


def angle_table(rows, cols, total):
    product = (
        jnp.arange(rows, dtype=jnp.int32)[:, None]
        * jnp.arange(cols, dtype=jnp.int32)[None, :]
        % total
    )
    angle = product.astype(jnp.float32) * (2.0 * math.pi / total)
    return (jnp.cos(angle), jnp.sin(angle))


def make_tables(length):
    second = length // 128
    cosine_first, sine_first = angle_table(128, 128, 128)
    cosine_second, sine_second = angle_table(second, second, second)
    cosine_twist, sine_twist = angle_table(128, second, length)
    return (
        cosine_first,
        sine_first,
        cosine_second,
        sine_second,
        cosine_twist[:, :, None],
        sine_twist[:, :, None],
    )


def across_first(matrix, array):
    return jnp.einsum(
        "kn,nmc->kmc", matrix, array, precision=table_mode, preferred_element_type=jnp.float32
    )


def across_second(array, matrix):
    return jnp.einsum(
        "kmc,ml->klc", array, matrix, precision=table_mode, preferred_element_type=jnp.float32
    )


def forward_transform(signal, tables):
    cosine_first, sine_first, cosine_second, sine_second, cosine_twist, sine_twist = tables
    half = cosine_first.shape[0] // 2
    shaped = signal.reshape(half, cosine_second.shape[0], signal.shape[1])
    real_section = across_first(cosine_first[:, :half], shaped)
    imag_section = -across_first(sine_first[:, :half], shaped)
    real_turned = real_section * cosine_twist + imag_section * sine_twist
    imag_turned = imag_section * cosine_twist - real_section * sine_twist
    real_out = across_second(real_turned, cosine_second) + across_second(imag_turned, sine_second)
    imag_out = across_second(imag_turned, cosine_second) - across_second(real_turned, sine_second)
    return (real_out, imag_out)


def inverse_transform(real_spec, imag_spec, tables):
    cosine_first, sine_first, cosine_second, sine_second, cosine_twist, sine_twist = tables
    half = cosine_first.shape[0] // 2
    total = cosine_first.shape[0] * cosine_second.shape[0]
    real_section = across_second(real_spec, cosine_second) - across_second(imag_spec, sine_second)
    imag_section = across_second(imag_spec, cosine_second) + across_second(real_spec, sine_second)
    real_turned = real_section * cosine_twist - imag_section * sine_twist
    imag_turned = imag_section * cosine_twist + real_section * sine_twist
    signal = (
        across_first(cosine_first[:half], real_turned)
        - across_first(sine_first[:half], imag_turned)
    ) / total
    return signal.reshape(half * cosine_second.shape[0], -1)


def spectral_tables(length):
    first = 128
    second = length // first
    half = first // 2
    cosine_first, sine_first = angle_table(first, first, first)
    cosine_second, sine_second = angle_table(second, second, second)
    cosine_twist, sine_twist = angle_table(first, second, length)
    forward_first = jnp.concatenate([cosine_first[:, :half], -sine_first[:, :half]], axis=0)
    forward_second = jnp.stack(
        [
            jnp.stack([cosine_second, -sine_second], axis=1),
            jnp.stack([sine_second, cosine_second], axis=1),
        ]
    )
    inverse_second = jnp.stack(
        [
            jnp.stack([cosine_second, sine_second], axis=1),
            jnp.stack([-sine_second, cosine_second], axis=1),
        ]
    )
    inverse_first = jnp.stack([cosine_first[:half], -sine_first[:half]], axis=1) / length
    return (
        forward_first,
        forward_second,
        inverse_second,
        inverse_first,
        cosine_twist[:, :, None],
        sine_twist[:, :, None],
    )


def spectra(signal, tables):
    forward_first, forward_second, _, _, cosine_twist, sine_twist = tables
    first = cosine_twist.shape[0]
    half = first // 2
    shaped = signal.reshape(half, cosine_twist.shape[1], signal.shape[1])
    section = jnp.einsum(
        "kn,nmc->kmc", forward_first, shaped, precision=table_mode,
        preferred_element_type=jnp.float32,
    )
    real_section, imag_section = section[:first], section[first:]
    turned = jnp.stack(
        [
            real_section * cosine_twist + imag_section * sine_twist,
            imag_section * cosine_twist - real_section * sine_twist,
        ]
    )
    return tuple(
        jnp.einsum(
            "rkmc,rml->klc", turned, forward_second[:, :, part], precision=table_mode,
            preferred_element_type=jnp.float32,
        )
        for part in range(2)
    )


def signals(spec, tables):
    _, _, inverse_second, inverse_first, cosine_twist, sine_twist = tables
    section = jnp.einsum(
        "sklc,slrm->rkmc", spec, inverse_second, precision=table_mode,
        preferred_element_type=jnp.float32,
    )
    real_section, imag_section = section[0], section[1]
    turned = jnp.stack(
        [
            real_section * cosine_twist - imag_section * sine_twist,
            imag_section * cosine_twist + real_section * sine_twist,
        ]
    )
    out = jnp.einsum(
        "nrk,rkmc->nmc", inverse_first, turned, precision=table_mode,
        preferred_element_type=jnp.float32,
    )
    return out.reshape(-1, out.shape[-1])


def shards(
    tokens, filter_taps, query_weight, key_weight, value_weight, output_weight, out_cotangent
):
    ctx = lax.axis_size("context")
    ten = lax.axis_size("tensor")
    rows = tokens.shape[1]
    arrived = lax.all_to_all(
        jnp.concatenate(
            [tokens[0], out_cotangent[0], filter_taps.astype(jnp.bfloat16)], axis=0
        ),
        "tensor",
        split_axis=1,
        concat_axis=0,
        tiled=True,
    )
    arrived = arrived.reshape(ten, 3, rows, arrived.shape[1])
    inputs = arrived[:, 0].reshape(ten * rows, -1)
    upstream = arrived[:, 1].reshape(ten * rows, -1)
    taps_mid = arrived[:, 2].reshape(ten * rows, -1)
    blocks = query_weight.shape[0]
    query = blockwise(inputs, query_weight).astype(jnp.bfloat16)
    keys = blockwise(inputs, key_weight).astype(jnp.bfloat16)
    values = blockwise(inputs, value_weight).astype(jnp.bfloat16)
    gated = (keys.astype(jnp.float32) * values.astype(jnp.float32)).astype(jnp.bfloat16)
    query_wide = query.astype(jnp.float32)
    back_weighted = blockwise_back(upstream, output_weight)
    conv_grad = (back_weighted * query_wide).astype(jnp.bfloat16)
    local = inputs.shape[0]
    gated_time, grad_time, taps = (
        lax.all_to_all(part, "context", split_axis=1, concat_axis=0, tiled=True)
        for part in (gated, conv_grad, taps_mid)
    )
    taps = taps.astype(jnp.float32)
    length = taps.shape[0]
    width = taps.shape[1]
    tables = spectral_tables(2 * length)
    spec = spectra(
        jnp.concatenate(
            [taps, gated_time.astype(jnp.float32), grad_time.astype(jnp.float32)], axis=1
        ),
        tables,
    )
    real_spec, imag_spec = spec
    real_taps, real_gated, real_grad = (
        real_spec[..., :width], real_spec[..., width : 2 * width], real_spec[..., 2 * width :]
    )
    imag_taps, imag_gated, imag_grad = (
        imag_spec[..., :width], imag_spec[..., width : 2 * width], imag_spec[..., 2 * width :]
    )
    products = jnp.stack(
        [
            jnp.concatenate(
                [
                    real_taps * real_gated - imag_taps * imag_gated,
                    real_taps * real_grad + imag_taps * imag_grad,
                    real_grad * real_gated + imag_grad * imag_gated,
                ],
                axis=-1,
            ),
            jnp.concatenate(
                [
                    real_taps * imag_gated + imag_taps * real_gated,
                    real_taps * imag_grad - imag_taps * real_grad,
                    imag_grad * real_gated - real_grad * imag_gated,
                ],
                axis=-1,
            ),
        ]
    )
    results = signals(products, tables)
    conv_time = results[:, :width]
    gated_time_back = results[:, width : 2 * width]
    taps_back = results[:, 2 * width :]
    returned = lax.all_to_all(
        jnp.stack(
            [
                conv_time.astype(jnp.bfloat16).reshape(ctx, local, width),
                gated_time_back.astype(jnp.bfloat16).reshape(ctx, local, width),
            ],
            axis=1,
        ).reshape(ctx * 2 * local, width),
        "context",
        split_axis=0,
        concat_axis=1,
        tiled=True,
    )
    conv, gated_narrow = lax.optimization_barrier((returned[:local], returned[local:]))
    conv_wide = conv.astype(jnp.float32)
    weighted = (query_wide * conv_wide).astype(jnp.bfloat16)
    query_back = (back_weighted * conv_wide).astype(jnp.bfloat16)
    gated_back = gated_narrow.astype(jnp.float32)
    key_back = (gated_back * values.astype(jnp.float32)).astype(jnp.bfloat16)
    value_back = (gated_back * keys.astype(jnp.float32)).astype(jnp.bfloat16)
    factor = 1.0 / math.sqrt(lax.axis_size("dp") * length)
    terms = (
        (weight_term(inputs, query_back, blocks) * factor).astype(jnp.bfloat16),
        (weight_term(inputs, key_back, blocks) * factor).astype(jnp.bfloat16),
        (weight_term(inputs, value_back, blocks) * factor).astype(jnp.bfloat16),
        (weight_term(weighted, upstream, blocks) * factor).astype(jnp.bfloat16),
    )
    terms, (query_back, key_back, value_back, weighted) = lax.optimization_barrier(
        (terms, (query_back, key_back, value_back, weighted))
    )
    query_grad, key_grad, value_grad, output_grad = (
        lax.psum(term, ("dp", "context")).astype(jnp.float32) for term in terms
    )
    mixed = blockwise(weighted, output_weight).astype(jnp.bfloat16)
    token_grad = (
        blockwise_back(query_back, query_weight)
        + blockwise_back(key_back, key_weight)
        + blockwise_back(value_back, value_weight)
    ).astype(jnp.bfloat16)
    taps_total = lax.psum((taps_back * factor).astype(jnp.bfloat16), "dp")
    filter_mid = lax.all_to_all(taps_total, "context", split_axis=0, concat_axis=1, tiled=True)
    leaving = lax.all_to_all(
        jnp.stack(
            [
                part.reshape(ten, rows, part.shape[1])
                for part in (mixed, token_grad, filter_mid)
            ],
            axis=1,
        ).reshape(ten * 3 * rows, -1),
        "tensor",
        split_axis=0,
        concat_axis=1,
        tiled=True,
    )
    mixed_rows = leaving[:rows]
    grad_rows = leaving[rows : 2 * rows]
    filter_grad = leaving[2 * rows :].astype(jnp.float32)
    return (
        mixed_rows[None],
        grad_rows[None],
        filter_grad,
        query_grad,
        key_grad,
        value_grad,
        output_grad,
    )


def solution(mesh):
    placed = (
        P("dp", ("context", "tensor"), None),
        P(("context", "tensor"), None),
        P("tensor", None, None),
        P("tensor", None, None),
        P("tensor", None, None),
        P("tensor", None, None),
        P("dp", ("context", "tensor"), None),
    )
    return jax.shard_map(
        shards,
        mesh=mesh,
        in_specs=placed,
        out_specs=(
            P("dp", ("context", "tensor"), None),
            P("dp", ("context", "tensor"), None),
            P(("context", "tensor"), None),
            P("tensor", None, None),
            P("tensor", None, None),
            P("tensor", None, None),
            P("tensor", None, None),
        ),
        check_vma=False,
    )
```

```python
import math

import jax
import jax.numpy as jnp
from jax import lax
from jax.sharding import PartitionSpec as P

table_mode = lax.Precision.DEFAULT


def blockwise(acts, weight):
    rows = acts.shape[0]
    shaped = acts.reshape(rows, weight.shape[0], weight.shape[1])
    return jnp.einsum("tni,nij->tnj", shaped, weight, preferred_element_type=jnp.float32).reshape(
        rows, -1
    )


def blockwise_back(acts, weight):
    rows = acts.shape[0]
    shaped = acts.reshape(rows, weight.shape[0], weight.shape[1])
    return jnp.einsum("tnj,nij->tni", shaped, weight, preferred_element_type=jnp.float32).reshape(
        rows, -1
    )


def weight_term(inputs, grads, blocks):
    rows = inputs.shape[0]
    left = inputs.reshape(rows, blocks, -1)
    right = grads.reshape(rows, blocks, -1)
    return jnp.einsum("tni,tnj->nij", left, right, preferred_element_type=jnp.float32)


def angle_table(rows, cols, total):
    product = (
        jnp.arange(rows, dtype=jnp.int32)[:, None]
        * jnp.arange(cols, dtype=jnp.int32)[None, :]
        % total
    )
    angle = product.astype(jnp.float32) * (2.0 * math.pi / total)
    return (jnp.cos(angle), jnp.sin(angle))


def make_tables(length):
    second = length // 128
    cosine_first, sine_first = angle_table(128, 128, 128)
    cosine_second, sine_second = angle_table(second, second, second)
    cosine_twist, sine_twist = angle_table(128, second, length)
    return (
        cosine_first,
        sine_first,
        cosine_second,
        sine_second,
        cosine_twist[:, :, None],
        sine_twist[:, :, None],
    )


def across_first(matrix, array):
    return jnp.einsum(
        "kn,nmc->kmc", matrix, array, precision=table_mode, preferred_element_type=jnp.float32
    )


def across_second(array, matrix):
    return jnp.einsum(
        "kmc,ml->klc", array, matrix, precision=table_mode, preferred_element_type=jnp.float32
    )


def forward_transform(signal, tables):
    cosine_first, sine_first, cosine_second, sine_second, cosine_twist, sine_twist = tables
    half = cosine_first.shape[0] // 2
    shaped = signal.reshape(half, cosine_second.shape[0], signal.shape[1])
    real_section = across_first(cosine_first[:, :half], shaped)
    imag_section = -across_first(sine_first[:, :half], shaped)
    real_turned = real_section * cosine_twist + imag_section * sine_twist
    imag_turned = imag_section * cosine_twist - real_section * sine_twist
    real_out = across_second(real_turned, cosine_second) + across_second(imag_turned, sine_second)
    imag_out = across_second(imag_turned, cosine_second) - across_second(real_turned, sine_second)
    return (real_out, imag_out)


def inverse_transform(real_spec, imag_spec, tables):
    cosine_first, sine_first, cosine_second, sine_second, cosine_twist, sine_twist = tables
    half = cosine_first.shape[0] // 2
    total = cosine_first.shape[0] * cosine_second.shape[0]
    real_section = across_second(real_spec, cosine_second) - across_second(imag_spec, sine_second)
    imag_section = across_second(imag_spec, cosine_second) + across_second(real_spec, sine_second)
    real_turned = real_section * cosine_twist - imag_section * sine_twist
    imag_turned = imag_section * cosine_twist + real_section * sine_twist
    signal = (
        across_first(cosine_first[:half], real_turned)
        - across_first(sine_first[:half], imag_turned)
    ) / total
    return signal.reshape(half * cosine_second.shape[0], -1)


def spectral_tables(length):
    first = 128
    second = length // first
    half = first // 2
    cosine_first, sine_first = angle_table(first, first, first)
    cosine_second, sine_second = angle_table(second, second, second)
    cosine_twist, sine_twist = angle_table(first, second, length)
    forward_first = jnp.concatenate([cosine_first[:, :half], -sine_first[:, :half]], axis=0)
    forward_second = jnp.stack(
        [
            jnp.stack([cosine_second, -sine_second], axis=1),
            jnp.stack([sine_second, cosine_second], axis=1),
        ]
    )
    inverse_second = jnp.stack(
        [
            jnp.stack([cosine_second, sine_second], axis=1),
            jnp.stack([-sine_second, cosine_second], axis=1),
        ]
    )
    inverse_first = jnp.stack([cosine_first[:half], -sine_first[:half]], axis=1) / length
    return (
        forward_first,
        forward_second,
        inverse_second,
        inverse_first,
        cosine_twist[:, :, None],
        sine_twist[:, :, None],
    )


def spectra(signal, tables):
    forward_first, forward_second, _, _, cosine_twist, sine_twist = tables
    first = cosine_twist.shape[0]
    half = first // 2
    shaped = signal.reshape(half, cosine_twist.shape[1], signal.shape[1])
    section = jnp.einsum(
        "kn,nmc->kmc", forward_first, shaped, precision=table_mode,
        preferred_element_type=jnp.float32,
    )
    real_section, imag_section = section[:first], section[first:]
    turned = jnp.stack(
        [
            real_section * cosine_twist + imag_section * sine_twist,
            imag_section * cosine_twist - real_section * sine_twist,
        ]
    )
    return tuple(
        jnp.einsum(
            "rkmc,rml->klc", turned, forward_second[:, :, part], precision=table_mode,
            preferred_element_type=jnp.float32,
        )
        for part in range(2)
    )


def signals(spec, tables):
    _, _, inverse_second, inverse_first, cosine_twist, sine_twist = tables
    section = jnp.einsum(
        "sklc,slrm->rkmc", spec, inverse_second, precision=table_mode,
        preferred_element_type=jnp.float32,
    )
    real_section, imag_section = section[0], section[1]
    turned = jnp.stack(
        [
            real_section * cosine_twist - imag_section * sine_twist,
            imag_section * cosine_twist + real_section * sine_twist,
        ]
    )
    out = jnp.einsum(
        "nrk,rkmc->nmc", inverse_first, turned, precision=table_mode,
        preferred_element_type=jnp.float32,
    )
    return out.reshape(-1, out.shape[-1])


def shards(
    tokens, filter_taps, query_weight, key_weight, value_weight, output_weight, out_cotangent
):
    ctx = lax.axis_size("context")
    ten = lax.axis_size("tensor")
    rows = tokens.shape[1]
    arrived = lax.all_to_all(
        jnp.concatenate(
            [tokens[0], out_cotangent[0], filter_taps.astype(jnp.bfloat16)], axis=0
        ),
        "tensor",
        split_axis=1,
        concat_axis=0,
        tiled=True,
    )
    arrived = arrived.reshape(ten, 3, rows, arrived.shape[1])
    inputs = arrived[:, 0].reshape(ten * rows, -1)
    upstream = arrived[:, 1].reshape(ten * rows, -1)
    taps_mid = arrived[:, 2].reshape(ten * rows, -1)
    blocks = query_weight.shape[0]
    query = blockwise(inputs, query_weight).astype(jnp.bfloat16)
    keys = blockwise(inputs, key_weight).astype(jnp.bfloat16)
    values = blockwise(inputs, value_weight).astype(jnp.bfloat16)
    gated = (keys.astype(jnp.float32) * values.astype(jnp.float32)).astype(jnp.bfloat16)
    query_wide = query.astype(jnp.float32)
    back_weighted = blockwise_back(upstream, output_weight)
    conv_grad = (back_weighted * query_wide).astype(jnp.bfloat16)
    local = inputs.shape[0]
    gated_time, grad_time, taps = (
        lax.all_to_all(part, "context", split_axis=1, concat_axis=0, tiled=True)
        for part in (gated, conv_grad, taps_mid)
    )
    taps = taps.astype(jnp.float32)
    length = taps.shape[0]
    width = taps.shape[1]
    tables = spectral_tables(2 * length)
    spec = spectra(
        jnp.concatenate(
            [taps, gated_time.astype(jnp.float32), grad_time.astype(jnp.float32)], axis=1
        ),
        tables,
    )
    real_spec, imag_spec = spec
    real_taps, real_gated, real_grad = (
        real_spec[..., :width], real_spec[..., width : 2 * width], real_spec[..., 2 * width :]
    )
    imag_taps, imag_gated, imag_grad = (
        imag_spec[..., :width], imag_spec[..., width : 2 * width], imag_spec[..., 2 * width :]
    )
    products = jnp.stack(
        [
            jnp.concatenate(
                [
                    real_taps * real_gated - imag_taps * imag_gated,
                    real_taps * real_grad + imag_taps * imag_grad,
                    real_grad * real_gated + imag_grad * imag_gated,
                ],
                axis=-1,
            ),
            jnp.concatenate(
                [
                    real_taps * imag_gated + imag_taps * real_gated,
                    real_taps * imag_grad - imag_taps * real_grad,
                    imag_grad * real_gated - real_grad * imag_gated,
                ],
                axis=-1,
            ),
        ]
    )
    results = signals(products, tables)
    conv_time = results[:, :width]
    gated_time_back = results[:, width : 2 * width]
    taps_back = results[:, 2 * width :]
    returned = lax.all_to_all(
        jnp.stack(
            [
                conv_time.astype(jnp.bfloat16).reshape(ctx, local, width),
                gated_time_back.astype(jnp.bfloat16).reshape(ctx, local, width),
            ],
            axis=1,
        ).reshape(ctx * 2 * local, width),
        "context",
        split_axis=0,
        concat_axis=1,
        tiled=True,
    )
    conv, gated_narrow = lax.optimization_barrier((returned[:local], returned[local:]))
    conv_wide = conv.astype(jnp.float32)
    weighted = (query_wide * conv_wide).astype(jnp.bfloat16)
    query_back = (back_weighted * conv_wide).astype(jnp.bfloat16)
    gated_back = gated_narrow.astype(jnp.float32)
    key_back = (gated_back * values.astype(jnp.float32)).astype(jnp.bfloat16)
    value_back = (gated_back * keys.astype(jnp.float32)).astype(jnp.bfloat16)
    factor = 1.0 / math.sqrt(lax.axis_size("dp") * length)
    terms = (
        (weight_term(inputs, query_back, blocks) * factor).astype(jnp.bfloat16),
        (weight_term(inputs, key_back, blocks) * factor).astype(jnp.bfloat16),
        (weight_term(inputs, value_back, blocks) * factor).astype(jnp.bfloat16),
        (weight_term(weighted, upstream, blocks) * factor).astype(jnp.bfloat16),
    )
    terms, (query_back, key_back, value_back, weighted) = lax.optimization_barrier(
        (terms, (query_back, key_back, value_back, weighted))
    )
    query_grad, key_grad, value_grad, output_grad = (
        lax.psum(term, ("dp", "context")).astype(jnp.float32) for term in terms
    )
    mixed = blockwise(weighted, output_weight).astype(jnp.bfloat16)
    token_grad = (
        blockwise_back(query_back, query_weight)
        + blockwise_back(key_back, key_weight)
        + blockwise_back(value_back, value_weight)
    ).astype(jnp.bfloat16)
    taps_total = lax.psum((taps_back * factor).astype(jnp.bfloat16), "dp")
    filter_mid = lax.all_to_all(taps_total, "context", split_axis=0, concat_axis=1, tiled=True)
    leaving = lax.all_to_all(
        jnp.stack(
            [
                part.reshape(ten, rows, part.shape[1])
                for part in (mixed, token_grad, filter_mid)
            ],
            axis=1,
        ).reshape(ten * 3 * rows, -1),
        "tensor",
        split_axis=0,
        concat_axis=1,
        tiled=True,
    )
    mixed_rows, grad_rows, filter_grad = lax.optimization_barrier(
        (leaving[:rows], leaving[rows : 2 * rows], leaving[2 * rows :])
    )
    filter_grad = filter_grad.astype(jnp.float32)
    return (
        mixed_rows[None],
        grad_rows[None],
        filter_grad,
        query_grad,
        key_grad,
        value_grad,
        output_grad,
    )


def solution(mesh):
    placed = (
        P("dp", ("context", "tensor"), None),
        P(("context", "tensor"), None),
        P("tensor", None, None),
        P("tensor", None, None),
        P("tensor", None, None),
        P("tensor", None, None),
        P("dp", ("context", "tensor"), None),
    )
    return jax.shard_map(
        shards,
        mesh=mesh,
        in_specs=placed,
        out_specs=(
            P("dp", ("context", "tensor"), None),
            P("dp", ("context", "tensor"), None),
            P(("context", "tensor"), None),
            P("tensor", None, None),
            P("tensor", None, None),
            P("tensor", None, None),
            P("tensor", None, None),
        ),
        check_vma=False,
    )
```

```python
import math

import jax
import jax.numpy as jnp
from jax import lax
from jax.sharding import PartitionSpec as P

table_mode = lax.Precision.DEFAULT


def blockwise(acts, weight):
    rows = acts.shape[0]
    shaped = acts.reshape(rows, weight.shape[0], weight.shape[1])
    return jnp.einsum("tni,nij->tnj", shaped, weight, preferred_element_type=jnp.float32).reshape(
        rows, -1
    )


def blockwise_back(acts, weight):
    rows = acts.shape[0]
    shaped = acts.reshape(rows, weight.shape[0], weight.shape[1])
    return jnp.einsum("tnj,nij->tni", shaped, weight, preferred_element_type=jnp.float32).reshape(
        rows, -1
    )


def weight_term(inputs, grads, blocks):
    rows = inputs.shape[0]
    left = inputs.reshape(rows, blocks, -1)
    right = grads.reshape(rows, blocks, -1)
    return jnp.einsum("tni,tnj->nij", left, right, preferred_element_type=jnp.float32)


def angle_table(rows, cols, total):
    product = (
        jnp.arange(rows, dtype=jnp.int32)[:, None]
        * jnp.arange(cols, dtype=jnp.int32)[None, :]
        % total
    )
    angle = product.astype(jnp.float32) * (2.0 * math.pi / total)
    return (jnp.cos(angle), jnp.sin(angle))


def make_tables(length):
    second = length // 128
    cosine_first, sine_first = angle_table(128, 128, 128)
    cosine_second, sine_second = angle_table(second, second, second)
    cosine_twist, sine_twist = angle_table(128, second, length)
    return (
        cosine_first,
        sine_first,
        cosine_second,
        sine_second,
        cosine_twist[:, :, None],
        sine_twist[:, :, None],
    )


def across_first(matrix, array):
    return jnp.einsum(
        "kn,nmc->kmc", matrix, array, precision=table_mode, preferred_element_type=jnp.float32
    )


def across_second(array, matrix):
    return jnp.einsum(
        "kmc,ml->klc", array, matrix, precision=table_mode, preferred_element_type=jnp.float32
    )


def forward_transform(signal, tables):
    cosine_first, sine_first, cosine_second, sine_second, cosine_twist, sine_twist = tables
    half = cosine_first.shape[0] // 2
    shaped = signal.reshape(half, cosine_second.shape[0], signal.shape[1])
    real_section = across_first(cosine_first[:, :half], shaped)
    imag_section = -across_first(sine_first[:, :half], shaped)
    real_turned = real_section * cosine_twist + imag_section * sine_twist
    imag_turned = imag_section * cosine_twist - real_section * sine_twist
    real_out = across_second(real_turned, cosine_second) + across_second(imag_turned, sine_second)
    imag_out = across_second(imag_turned, cosine_second) - across_second(real_turned, sine_second)
    return (real_out, imag_out)


def inverse_transform(real_spec, imag_spec, tables):
    cosine_first, sine_first, cosine_second, sine_second, cosine_twist, sine_twist = tables
    half = cosine_first.shape[0] // 2
    total = cosine_first.shape[0] * cosine_second.shape[0]
    real_section = across_second(real_spec, cosine_second) - across_second(imag_spec, sine_second)
    imag_section = across_second(imag_spec, cosine_second) + across_second(real_spec, sine_second)
    real_turned = real_section * cosine_twist - imag_section * sine_twist
    imag_turned = imag_section * cosine_twist + real_section * sine_twist
    signal = (
        across_first(cosine_first[:half], real_turned)
        - across_first(sine_first[:half], imag_turned)
    ) / total
    return signal.reshape(half * cosine_second.shape[0], -1)


def spectral_tables(length):
    first = 128
    second = length // first
    half = first // 2
    cosine_first, sine_first = angle_table(first, first, first)
    cosine_second, sine_second = angle_table(second, second, second)
    cosine_twist, sine_twist = angle_table(first, second, length)
    forward_first = jnp.concatenate([cosine_first[:, :half], -sine_first[:, :half]], axis=0)
    forward_second = jnp.stack(
        [
            jnp.stack([cosine_second, -sine_second], axis=1),
            jnp.stack([sine_second, cosine_second], axis=1),
        ]
    )
    inverse_second = jnp.stack(
        [
            jnp.stack([cosine_second, sine_second], axis=1),
            jnp.stack([-sine_second, cosine_second], axis=1),
        ]
    )
    inverse_first = jnp.stack([cosine_first[:half], -sine_first[:half]], axis=1) / length
    return (
        forward_first,
        forward_second,
        inverse_second,
        inverse_first,
        cosine_twist[:, :, None],
        sine_twist[:, :, None],
    )


def spectra(signal, tables):
    forward_first, forward_second, _, _, cosine_twist, sine_twist = tables
    first = cosine_twist.shape[0]
    half = first // 2
    shaped = signal.reshape(half, cosine_twist.shape[1], signal.shape[1])
    section = jnp.einsum(
        "kn,nmc->kmc", forward_first, shaped, precision=table_mode,
        preferred_element_type=jnp.float32,
    )
    real_section, imag_section = section[:first], section[first:]
    turned = jnp.stack(
        [
            real_section * cosine_twist + imag_section * sine_twist,
            imag_section * cosine_twist - real_section * sine_twist,
        ]
    )
    return tuple(
        jnp.einsum(
            "rkmc,rml->klc", turned, forward_second[:, :, part], precision=table_mode,
            preferred_element_type=jnp.float32,
        )
        for part in range(2)
    )


def signals(spec, tables):
    _, _, inverse_second, inverse_first, cosine_twist, sine_twist = tables
    section = jnp.einsum(
        "sklc,slrm->rkmc", spec, inverse_second, precision=table_mode,
        preferred_element_type=jnp.float32,
    )
    real_section, imag_section = section[0], section[1]
    turned = jnp.stack(
        [
            real_section * cosine_twist - imag_section * sine_twist,
            imag_section * cosine_twist + real_section * sine_twist,
        ]
    )
    out = jnp.einsum(
        "nrk,rkmc->nmc", inverse_first, turned, precision=table_mode,
        preferred_element_type=jnp.float32,
    )
    return out.reshape(-1, out.shape[-1])


def shards(
    tokens, filter_taps, query_weight, key_weight, value_weight, output_weight, out_cotangent
):
    ctx = lax.axis_size("context")
    ten = lax.axis_size("tensor")
    rows = tokens.shape[1]
    arrived = lax.all_to_all(
        jnp.concatenate(
            [tokens[0], out_cotangent[0], filter_taps.astype(jnp.bfloat16)], axis=0
        ),
        "tensor",
        split_axis=1,
        concat_axis=0,
        tiled=True,
    )
    arrived = arrived.reshape(ten, 3, rows, arrived.shape[1])
    inputs = arrived[:, 0].reshape(ten * rows, -1)
    upstream = arrived[:, 1].reshape(ten * rows, -1)
    taps_mid = arrived[:, 2].reshape(ten * rows, -1)
    blocks = query_weight.shape[0]
    query = blockwise(inputs, query_weight).astype(jnp.bfloat16)
    keys = blockwise(inputs, key_weight).astype(jnp.bfloat16)
    values = blockwise(inputs, value_weight).astype(jnp.bfloat16)
    gated = (keys.astype(jnp.float32) * values.astype(jnp.float32)).astype(jnp.bfloat16)
    query_wide = query.astype(jnp.float32)
    back_weighted = blockwise_back(upstream, output_weight)
    conv_grad = (back_weighted * query_wide).astype(jnp.bfloat16)
    local = inputs.shape[0]
    gated_time, grad_time, taps = (
        lax.all_to_all(part, "context", split_axis=1, concat_axis=0, tiled=True)
        for part in (gated, conv_grad, taps_mid)
    )
    taps = taps.astype(jnp.float32)
    length = taps.shape[0]
    width = taps.shape[1]
    tables = spectral_tables(2 * length)
    spec = spectra(
        jnp.concatenate(
            [taps, gated_time.astype(jnp.float32), grad_time.astype(jnp.float32)], axis=1
        ),
        tables,
    )
    real_spec, imag_spec = spec
    real_taps, real_gated, real_grad = (
        real_spec[..., :width], real_spec[..., width : 2 * width], real_spec[..., 2 * width :]
    )
    imag_taps, imag_gated, imag_grad = (
        imag_spec[..., :width], imag_spec[..., width : 2 * width], imag_spec[..., 2 * width :]
    )
    products = jnp.stack(
        [
            jnp.concatenate(
                [
                    real_taps * real_gated - imag_taps * imag_gated,
                    real_taps * real_grad + imag_taps * imag_grad,
                    real_grad * real_gated + imag_grad * imag_gated,
                ],
                axis=-1,
            ),
            jnp.concatenate(
                [
                    real_taps * imag_gated + imag_taps * real_gated,
                    real_taps * imag_grad - imag_taps * real_grad,
                    imag_grad * real_gated - real_grad * imag_gated,
                ],
                axis=-1,
            ),
        ]
    )
    results = signals(products, tables)
    conv_time, gated_time_back = lax.optimization_barrier(
        (results[:, :width].astype(jnp.bfloat16), results[:, width : 2 * width].astype(jnp.bfloat16))
    )
    taps_back = results[:, 2 * width :]
    returned = lax.all_to_all(
        jnp.stack(
            [
                conv_time.astype(jnp.bfloat16).reshape(ctx, local, width),
                gated_time_back.astype(jnp.bfloat16).reshape(ctx, local, width),
            ],
            axis=1,
        ).reshape(ctx * 2 * local, width),
        "context",
        split_axis=0,
        concat_axis=1,
        tiled=True,
    )
    conv, gated_narrow = lax.optimization_barrier((returned[:local], returned[local:]))
    conv_wide = conv.astype(jnp.float32)
    weighted = (query_wide * conv_wide).astype(jnp.bfloat16)
    query_back = (back_weighted * conv_wide).astype(jnp.bfloat16)
    gated_back = gated_narrow.astype(jnp.float32)
    key_back = (gated_back * values.astype(jnp.float32)).astype(jnp.bfloat16)
    value_back = (gated_back * keys.astype(jnp.float32)).astype(jnp.bfloat16)
    factor = 1.0 / math.sqrt(lax.axis_size("dp") * length)
    terms = (
        (weight_term(inputs, query_back, blocks) * factor).astype(jnp.bfloat16),
        (weight_term(inputs, key_back, blocks) * factor).astype(jnp.bfloat16),
        (weight_term(inputs, value_back, blocks) * factor).astype(jnp.bfloat16),
        (weight_term(weighted, upstream, blocks) * factor).astype(jnp.bfloat16),
    )
    terms, (query_back, key_back, value_back, weighted) = lax.optimization_barrier(
        (terms, (query_back, key_back, value_back, weighted))
    )
    query_grad, key_grad, value_grad, output_grad = (
        lax.psum(term, ("dp", "context")).astype(jnp.float32) for term in terms
    )
    mixed = blockwise(weighted, output_weight).astype(jnp.bfloat16)
    token_grad = (
        blockwise_back(query_back, query_weight)
        + blockwise_back(key_back, key_weight)
        + blockwise_back(value_back, value_weight)
    ).astype(jnp.bfloat16)
    taps_total = lax.psum((taps_back * factor).astype(jnp.bfloat16), "dp")
    filter_mid = lax.all_to_all(taps_total, "context", split_axis=0, concat_axis=1, tiled=True)
    leaving = lax.all_to_all(
        jnp.stack(
            [
                part.reshape(ten, rows, part.shape[1])
                for part in (mixed, token_grad, filter_mid)
            ],
            axis=1,
        ).reshape(ten * 3 * rows, -1),
        "tensor",
        split_axis=0,
        concat_axis=1,
        tiled=True,
    )
    mixed_rows, grad_rows, filter_grad = lax.optimization_barrier(
        (leaving[:rows], leaving[rows : 2 * rows], leaving[2 * rows :])
    )
    filter_grad = filter_grad.astype(jnp.float32)
    return (
        mixed_rows[None],
        grad_rows[None],
        filter_grad,
        query_grad,
        key_grad,
        value_grad,
        output_grad,
    )


def solution(mesh):
    placed = (
        P("dp", ("context", "tensor"), None),
        P(("context", "tensor"), None),
        P("tensor", None, None),
        P("tensor", None, None),
        P("tensor", None, None),
        P("tensor", None, None),
        P("dp", ("context", "tensor"), None),
    )
    return jax.shard_map(
        shards,
        mesh=mesh,
        in_specs=placed,
        out_specs=(
            P("dp", ("context", "tensor"), None),
            P("dp", ("context", "tensor"), None),
            P(("context", "tensor"), None),
            P("tensor", None, None),
            P("tensor", None, None),
            P("tensor", None, None),
            P("tensor", None, None),
        ),
        check_vma=False,
    )
```
